256 devices in a mesh: lat: 16 (over y_lo, z), lon: 16 (over y_hi, x, core).
Axes of the slice: x: 4, y: 4 (y_hi: 2, y_lo: 2; y = y_hi * 2 + y_lo), z: 8, core: 2. Of those that a mesh axis runs over, the one named last changes fastest.
Arguments:
- prognostic: float32 [6, 2, 2304, 2048], P(None, None, 'lon', 'lat'), may hold values from -6 to 6
- wind_zonal: float32 [2, 2048], P(None, 'lat'), may hold values from -1 to 1
- wind_merid: float32 [2, 2048], P(None, 'lat'), may hold values from -0.5 to 0.5
- layer_depth: float32 [2], replicated, may hold values from 0.25 to 1
- diffusion: float32 [3, 2], replicated, may hold values from 0.05 to 0.4
Outputs:
- prognostic_out: float32 [6, 2, 2304, 2048], P(None, None, 'lon', 'lat')
The draws below stay inside these ranges and needn't reach their ends.
All inputs are finite; a program needn't handle non-finite values.
Results may differ from the reference program's by a relative error of at most 0.00013.
Values sent between devices are 32-bit elements; how exact they have to be, the bound alone decides.
No kernel may reach another device: no remote copies, remote signals or barrier semaphores. Data moves between devices by JAX's collectives and lax.ppermute only.
A program may use at most 128 MiB of HBM per device.

```python
import math
import jax
import jax.numpy as jnp

NLON = 2304
FIELDS = 6
LEV = 2
ITERS = 3
NLAT = 2048


def levels(key, dims, split, smallest, largest):
    gain, own = 1.0, jax.random.fold_in(key, 6)
    for axis_at, shards_of in split:
        heights = jnp.exp(jax.random.uniform(jax.random.fold_in(own, axis_at), (shards_of,), jnp.float32, smallest / len(split), largest / len(split)))
        gain = gain * jnp.repeat(heights, dims[axis_at] // shards_of).reshape([-1 if axis == axis_at else 1 for axis in range(len(dims))])
    return gain


def noise(stream_key, extent, spread, reach, shards=(), held_as=jnp.bfloat16):
    drawn = spread * jax.random.normal(stream_key, extent, jnp.float32)
    if shards:
        drawn = drawn * levels(stream_key, extent, shards, -0.22, 0.18)
    return jnp.clip(drawn, -reach, reach).astype(held_as)


def setup_inputs(seed: int = 0) -> dict:
    arg_keys = jax.random.split(jax.random.key(seed), 6)
    return {
        "prognostic": noise(arg_keys[0], (FIELDS, LEV, NLON, NLAT), 1.0, 6.0, ((2, 16), (3, 16)), jnp.float32),
        "wind_zonal": jnp.clip(jax.random.uniform(arg_keys[1], (LEV, NLAT), jnp.float32, -1.0, 1.0) * levels(arg_keys[1], (LEV, NLAT), ((1, 16),), -0.4, 0.0), -1.0, 1.0),
        "wind_merid": jnp.clip(jax.random.uniform(arg_keys[2], (LEV, NLAT), jnp.float32, -0.5, 0.5) * levels(arg_keys[2], (LEV, NLAT), ((1, 16),), -0.4, 0.0), -0.5, 0.5),
        "layer_depth": jnp.clip(jnp.exp(jax.random.uniform(arg_keys[3], (LEV,), jnp.float32, math.log(0.25), math.log(1.0))), 0.25, 1.0),
        "diffusion": jnp.clip(jnp.exp(jax.random.uniform(arg_keys[4], (3, LEV), jnp.float32, math.log(0.05), math.log(0.4))), 0.05, 0.4),
    }


time_step = 0.15


def latitude(row_ids, lat_total):
    return (row_ids.astype(jnp.float32) + 0.5) * (math.pi / lat_total) - 0.5 * math.pi


def damping(row_ids, lat_total, circle_len):
    cos_ratio = jnp.cos(latitude(row_ids, lat_total)) / math.cos(0.25 * math.pi)
    wave_ids = jnp.arange(circle_len // 2 + 1)
    sine_vals = jnp.sin(wave_ids.astype(jnp.float32) * (math.pi / circle_len))
    safe_sines = jnp.where(wave_ids == 0, 1.0, sine_vals)
    return jnp.where(wave_ids[None, :] == 0, 1.0, jnp.minimum(1.0, cos_ratio[:, None] / safe_sines[None, :]))


def tendency(fields_now, north_rows, south_rows, east_cols, west_cols, row_ids, lat_total, wind_zonal, wind_merid, layer_depth, diffusion):
    latitudes = latitude(row_ids, lat_total)
    cos_centre = jnp.cos(latitudes)
    cos_north = jnp.cos(latitude(row_ids + 1, lat_total))
    cos_south = jnp.cos(latitude(row_ids - 1, lat_total))
    coriolis = jnp.sin(latitudes)
    zonal_diff = (east_cols - west_cols) / (2.0 * cos_centre)
    merid_diff = 0.5 * (north_rows - south_rows)
    advect = wind_zonal[:, None, :] * zonal_diff + wind_merid[:, None, :] * merid_diff
    diverge = zonal_diff[0] + (north_rows[1] * cos_north - south_rows[1] * cos_south) / (2.0 * cos_centre)
    zonal_tend = -advect[0] + coriolis * fields_now[1] - zonal_diff[2]
    merid_tend = -advect[1] - coriolis * fields_now[0] - merid_diff[2]
    height_tend = -advect[2] - layer_depth[:, None, None] * diverge
    tracer_tend = -advect[3:] + diffusion[:, :, None, None] * (north_rows[3:] - 2.0 * fields_now[3:] + south_rows[3:])
    return jnp.concatenate([zonal_tend[None], merid_tend[None], height_tend[None], tracer_tend], axis=0)


def reference(prognostic, wind_zonal, wind_merid, layer_depth, diffusion):
    row_ids = jnp.arange(NLAT)
    damp_table = jnp.transpose(damping(row_ids, NLAT, NLON))
    fields_now = prognostic
    for substep in range(ITERS):
        lat_padded = jnp.pad(fields_now, ((0, 0), (0, 0), (0, 0), (1, 1)))
        east_cols = jnp.roll(fields_now, -1, axis=2)
        west_cols = jnp.roll(fields_now, 1, axis=2)
        tendency_now = tendency(fields_now, lat_padded[:, :, :, 2:], lat_padded[:, :, :, :-2], east_cols, west_cols, row_ids, NLAT, wind_zonal, wind_merid, layer_depth, diffusion)
        spectrum = jnp.fft.rfft(tendency_now, axis=2)
        filtered = jnp.fft.irfft(spectrum * damp_table, n=NLON, axis=2)
        fields_now = fields_now + time_step * filtered
    return fields_now
```

```python
import math

import jax
import jax.numpy as jnp
from jax import lax
from jax.sharding import PartitionSpec as P

ITERS = 3


time_step = 0.15
highest = lax.Precision.HIGHEST


def with_halo(block, sides, width, periodic):
    for axis, dim in sides:
        count = lax.axis_size(axis)
        forward = [(i, i + 1) for i in range(count - 1)]
        if periodic:
            forward.append((count - 1, 0))
        backward = [(target, source) for source, target in forward]
        low = lax.ppermute(
            lax.slice_in_dim(block, block.shape[dim] - width, None, axis=dim), axis, forward
        )
        high = lax.ppermute(lax.slice_in_dim(block, 0, width, axis=dim), axis, backward)
        block = jnp.concatenate([low, block, high], axis=dim)
    return block


def latitude(row_ids, lat_total):
    return (row_ids.astype(jnp.float32) + 0.5) * (math.pi / lat_total) - 0.5 * math.pi


def damping(row_ids, lat_total, circle_len):
    cos_ratio = jnp.cos(latitude(row_ids, lat_total)) / math.cos(0.25 * math.pi)
    wave_ids = jnp.arange(circle_len // 2 + 1)
    sine_vals = jnp.sin(wave_ids.astype(jnp.float32) * (math.pi / circle_len))
    safe_sines = jnp.where(wave_ids == 0, 1.0, sine_vals)
    return jnp.where(
        wave_ids[None, :] == 0, 1.0, jnp.minimum(1.0, cos_ratio[:, None] / safe_sines[None, :])
    )


def tendency(
    fields_now,
    north_rows,
    south_rows,
    east_cols,
    west_cols,
    row_ids,
    lat_total,
    wind_zonal,
    wind_merid,
    layer_depth,
    diffusion,
):
    latitudes = latitude(row_ids, lat_total)
    cos_centre = jnp.cos(latitudes)
    cos_north = jnp.cos(latitude(row_ids + 1, lat_total))
    cos_south = jnp.cos(latitude(row_ids - 1, lat_total))
    coriolis = jnp.sin(latitudes)
    zonal_diff = (east_cols - west_cols) / (2.0 * cos_centre)
    merid_diff = 0.5 * (north_rows - south_rows)
    advect = wind_zonal[:, None, :] * zonal_diff + wind_merid[:, None, :] * merid_diff
    diverge = zonal_diff[0] + (north_rows[1] * cos_north - south_rows[1] * cos_south) / (
        2.0 * cos_centre
    )
    zonal_tend = -advect[0] + coriolis * fields_now[1] - zonal_diff[2]
    merid_tend = -advect[1] - coriolis * fields_now[0] - merid_diff[2]
    height_tend = -advect[2] - layer_depth[:, None, None] * diverge
    tracer_tend = -advect[3:] + diffusion[:, :, None, None] * (
        north_rows[3:] - 2.0 * fields_now[3:] + south_rows[3:]
    )
    return jnp.concatenate(
        [zonal_tend[None], merid_tend[None], height_tend[None], tracer_tend], axis=0
    )


def trig_pair(rows, cols, length, sign):
    phases = (
        jnp.arange(rows, dtype=jnp.int32)[:, None] * jnp.arange(cols, dtype=jnp.int32)[None, :]
    ) % length
    angles = phases.astype(jnp.float32) * (2.0 * math.pi / length)
    return jnp.cos(angles), sign * jnp.sin(angles)


def mm(table, data, spec):
    return jnp.einsum(spec, table, data, precision=highest)


def filter_circles(sector, factors, devs, local):
    total = devs * local
    c16, s16 = trig_pair(devs, devs, devs, -1.0)
    cm, sm = trig_pair(local, local, local, -1.0)
    tw_c, tw_s = trig_pair(devs, local, total, -1.0)
    tw_c = tw_c[:, :, None]
    tw_s = tw_s[:, :, None]
    a_re = mm(c16, sector, "ks,smc->kmc")
    a_im = mm(s16, sector, "ks,smc->kmc")
    b_re = a_re * tw_c - a_im * tw_s
    b_im = a_re * tw_s + a_im * tw_c
    x_re = mm(cm, b_re, "qm,kmc->kqc") - mm(sm, b_im, "qm,kmc->kqc")
    x_im = mm(cm, b_im, "qm,kmc->kqc") + mm(sm, b_re, "qm,kmc->kqc")
    y_re = x_re * factors
    y_im = x_im * factors
    d_re = mm(cm, y_re, "mq,kqc->kmc") + mm(sm, y_im, "mq,kqc->kmc")
    d_im = mm(cm, y_im, "mq,kqc->kmc") - mm(sm, y_re, "mq,kqc->kmc")
    e_re = d_re * tw_c + d_im * tw_s
    e_im = d_im * tw_c - d_re * tw_s
    out = mm(c16, e_re, "sk,kmc->smc") + mm(s16, e_im, "sk,kmc->smc")
    return out * (1.0 / total)


def local(prognostic, wind_zonal, wind_merid, layer_depth, diffusion):
    field_count, level_count, col_count, row_count = prognostic.shape
    lat_devs = lax.axis_size("lat")
    lon_devs = lax.axis_size("lon")
    lat_total = row_count * lat_devs
    circle_len = col_count * lon_devs
    lat_pos = lax.axis_index("lat")
    lon_pos = lax.axis_index("lon")
    row_ids = lat_pos * row_count + jnp.arange(row_count, dtype=jnp.int32)
    quarter = lat_devs // 4
    is_polar = (lat_pos < quarter) | (lat_pos >= lat_devs - quarter)
    vectors = field_count * level_count
    slab_rows = row_count // lon_devs
    circles = vectors * slab_rows

    start_row = lat_pos * row_count + lon_pos * slab_rows
    halfway = damping(start_row + jnp.arange(slab_rows, dtype=jnp.int32), lat_total, circle_len)
    mirrored = halfway[:, 1 : circle_len // 2][:, ::-1]
    full = jnp.concatenate([halfway, mirrored], axis=1)
    by_k = full.reshape(slab_rows, col_count, lon_devs)
    by_k = jnp.transpose(by_k, (2, 1, 0))
    factors = jnp.broadcast_to(
        by_k[:, :, None, :], (lon_devs, col_count, vectors, slab_rows)
    ).reshape(lon_devs, col_count, circles)

    def exchange_and_filter(flat):
        send = flat.reshape(vectors, col_count, lon_devs, slab_rows)
        send = jnp.transpose(send, (2, 1, 0, 3)).reshape(lon_devs, col_count, circles)
        recv = lax.all_to_all(send, "lon", 0, 0, tiled=True)
        smoothed = filter_circles(recv, factors, lon_devs, col_count)
        back = lax.all_to_all(smoothed, "lon", 0, 0, tiled=True)
        back = back.reshape(lon_devs, col_count, vectors, slab_rows)
        return jnp.transpose(back, (2, 1, 0, 3)).reshape(vectors, col_count, row_count)

    fields_now = prognostic
    for substep in range(ITERS):
        lat_padded = with_halo(fields_now, (("lat", 3),), 1, False)
        lon_padded = with_halo(fields_now, (("lon", 2),), 1, True)
        tendency_now = tendency(
            fields_now,
            lat_padded[:, :, :, 2:],
            lat_padded[:, :, :, :-2],
            lon_padded[:, :, 2:],
            lon_padded[:, :, :-2],
            row_ids,
            lat_total,
            wind_zonal,
            wind_merid,
            layer_depth,
            diffusion,
        )
        flattened = tendency_now.reshape(vectors, col_count, row_count)
        filtered = lax.cond(is_polar, exchange_and_filter, lambda inner: inner, flattened)
        fields_now = fields_now + time_step * filtered.reshape(fields_now.shape)
    return fields_now


def solution(mesh):
    return jax.shard_map(
        local,
        mesh=mesh,
        in_specs=(P(None, None, "lon", "lat"), P(None, "lat"), P(None, "lat"), P(), P()),
        out_specs=P(None, None, "lon", "lat"),
        check_vma=False,
    )
```

```python
import math

import jax
import jax.numpy as jnp
from jax import lax
from jax.sharding import PartitionSpec as P

ITERS = 3


time_step = 0.15
highest = lax.Precision.HIGHEST


def latitude(row_ids, lat_total):
    return (row_ids.astype(jnp.float32) + 0.5) * (math.pi / lat_total) - 0.5 * math.pi


def damping(row_ids, lat_total, circle_len):
    cos_ratio = jnp.cos(latitude(row_ids, lat_total)) / math.cos(0.25 * math.pi)
    wave_ids = jnp.arange(circle_len // 2 + 1)
    sine_vals = jnp.sin(wave_ids.astype(jnp.float32) * (math.pi / circle_len))
    safe_sines = jnp.where(wave_ids == 0, 1.0, sine_vals)
    return jnp.where(
        wave_ids[None, :] == 0, 1.0, jnp.minimum(1.0, cos_ratio[:, None] / safe_sines[None, :])
    )


def tendency(
    fields_now,
    north_rows,
    south_rows,
    east_cols,
    west_cols,
    row_ids,
    lat_total,
    wind_zonal,
    wind_merid,
    layer_depth,
    diffusion,
):
    latitudes = latitude(row_ids, lat_total)
    cos_centre = jnp.cos(latitudes)
    cos_north = jnp.cos(latitude(row_ids + 1, lat_total))
    cos_south = jnp.cos(latitude(row_ids - 1, lat_total))
    coriolis = jnp.sin(latitudes)
    zonal_diff = (east_cols - west_cols) / (2.0 * cos_centre)
    merid_diff = 0.5 * (north_rows - south_rows)
    advect = wind_zonal[:, None, :] * zonal_diff + wind_merid[:, None, :] * merid_diff
    diverge = zonal_diff[0] + (north_rows[1] * cos_north - south_rows[1] * cos_south) / (
        2.0 * cos_centre
    )
    zonal_tend = -advect[0] + coriolis * fields_now[1] - zonal_diff[2]
    merid_tend = -advect[1] - coriolis * fields_now[0] - merid_diff[2]
    height_tend = -advect[2] - layer_depth[:, None, None] * diverge
    tracer_tend = -advect[3:] + diffusion[:, :, None, None] * (
        north_rows[3:] - 2.0 * fields_now[3:] + south_rows[3:]
    )
    return jnp.concatenate(
        [zonal_tend[None], merid_tend[None], height_tend[None], tracer_tend], axis=0
    )


def trig_pair(rows, cols, length):
    phases = (
        jnp.arange(rows, dtype=jnp.int32)[:, None] * jnp.arange(cols, dtype=jnp.int32)[None, :]
    ) % length
    angles = phases.astype(jnp.float32) * (2.0 * math.pi / length)
    return jnp.cos(angles), jnp.sin(angles)


def mm(table, data, spec):
    return jnp.einsum(spec, table, data, precision=highest)


def filter_circles(flat, factors, devs, local, circles):
    total = devs * local
    c16, s16 = trig_pair(devs, devs, devs)
    cm, sm = trig_pair(local, local, local)
    tw_c, tw_s = trig_pair(devs, local, total)
    tw_c = tw_c[:, :, None]
    tw_s = tw_s[:, :, None]
    first = jnp.concatenate([c16, -s16], axis=0)
    last = jnp.concatenate([c16, -s16], axis=1) * (1.0 / total)
    fwd = jnp.concatenate(
        [jnp.concatenate([cm, sm], axis=1), jnp.concatenate([-sm, cm], axis=1)], axis=0
    )
    inv = jnp.concatenate(
        [jnp.concatenate([cm, -sm], axis=1), jnp.concatenate([sm, cm], axis=1)], axis=0
    )
    a = mm(first, flat, "ks,sf->kf").reshape(2, devs, local, circles)
    b_re = a[0] * tw_c + a[1] * tw_s
    b_im = a[1] * tw_c - a[0] * tw_s
    b = jnp.stack([b_re, b_im], axis=1).reshape(devs, 2 * local, circles)
    x = mm(fwd, b, "qp,kpc->kqc") * factors
    d = mm(inv, x, "mq,kqc->kmc").reshape(devs, 2, local, circles)
    e_re = d[:, 0] * tw_c - d[:, 1] * tw_s
    e_im = d[:, 1] * tw_c + d[:, 0] * tw_s
    e = jnp.stack([e_re, e_im], axis=0).reshape(2 * devs, local * circles)
    return mm(last, e, "sk,kf->sf")


def lat_halo(block, axis):
    count = lax.axis_size(axis)
    shape = block.shape
    compact = (shape[0] * shape[1], shape[2])
    up = [(i, i + 1) for i in range(count - 1)]
    down = [(i + 1, i) for i in range(count - 1)]
    south = lax.ppermute(block[:, :, :, -1].reshape(compact), axis, up)
    north = lax.ppermute(block[:, :, :, 0].reshape(compact), axis, down)
    south = south.reshape(shape[0], shape[1], shape[2], 1)
    north = north.reshape(shape[0], shape[1], shape[2], 1)
    north_rows = jnp.concatenate([block[:, :, :, 1:], north], axis=3)
    south_rows = jnp.concatenate([south, block[:, :, :, :-1]], axis=3)
    return north_rows, south_rows


def lon_halo(block, axis):
    count = lax.axis_size(axis)
    shape = block.shape
    compact = (shape[0] * shape[1], shape[3])
    up = [(i, (i + 1) % count) for i in range(count)]
    down = [((i + 1) % count, i) for i in range(count)]
    west = lax.ppermute(block[:, :, -1, :].reshape(compact), axis, up)
    east = lax.ppermute(block[:, :, 0, :].reshape(compact), axis, down)
    west = west.reshape(shape[0], shape[1], 1, shape[3])
    east = east.reshape(shape[0], shape[1], 1, shape[3])
    east_cols = jnp.concatenate([block[:, :, 1:], east], axis=2)
    west_cols = jnp.concatenate([west, block[:, :, :-1]], axis=2)
    return east_cols, west_cols


def local(prognostic, wind_zonal, wind_merid, layer_depth, diffusion):
    field_count, level_count, col_count, row_count = prognostic.shape
    lat_devs = lax.axis_size("lat")
    lon_devs = lax.axis_size("lon")
    lat_total = row_count * lat_devs
    circle_len = col_count * lon_devs
    lat_pos = lax.axis_index("lat")
    lon_pos = lax.axis_index("lon")
    row_ids = lat_pos * row_count + jnp.arange(row_count, dtype=jnp.int32)
    quarter = lat_devs // 4
    is_polar = (lat_pos < quarter) | (lat_pos >= lat_devs - quarter)
    vectors = field_count * level_count
    slab_rows = row_count // lon_devs
    circles = vectors * slab_rows
    chunk = col_count * circles
    lanes = 128 if chunk % 128 == 0 else chunk

    start_row = lat_pos * row_count + lon_pos * slab_rows
    halfway = damping(start_row + jnp.arange(slab_rows, dtype=jnp.int32), lat_total, circle_len)
    mirrored = halfway[:, 1 : circle_len // 2][:, ::-1]
    full = jnp.concatenate([halfway, mirrored], axis=1)
    by_k = full.reshape(slab_rows, col_count, lon_devs)
    by_k = jnp.transpose(by_k, (2, 1, 0))
    factors = jnp.broadcast_to(
        by_k[:, None, :, None, :], (lon_devs, 2, col_count, vectors, slab_rows)
    ).reshape(lon_devs, 2 * col_count, circles)

    def exchange_and_filter(flat):
        send = flat.reshape(vectors, col_count, lon_devs, slab_rows)
        send = jnp.transpose(send, (2, 1, 0, 3)).reshape(lon_devs, chunk // lanes, lanes)
        recv = lax.all_to_all(send, "lon", 0, 0, tiled=True).reshape(lon_devs, chunk)
        smoothed = filter_circles(recv, factors, lon_devs, col_count, circles)
        back = lax.all_to_all(smoothed.reshape(lon_devs, chunk // lanes, lanes), "lon", 0, 0, tiled=True)
        back = back.reshape(lon_devs, col_count, vectors, slab_rows)
        return jnp.transpose(back, (2, 1, 0, 3)).reshape(vectors, col_count, row_count)

    fields_now = prognostic
    for substep in range(ITERS):
        north_rows, south_rows = lat_halo(fields_now, "lat")
        east_cols, west_cols = lon_halo(fields_now, "lon")
        tendency_now = tendency(
            fields_now,
            north_rows,
            south_rows,
            east_cols,
            west_cols,
            row_ids,
            lat_total,
            wind_zonal,
            wind_merid,
            layer_depth,
            diffusion,
        )
        flattened = tendency_now.reshape(vectors, col_count, row_count)
        filtered = lax.cond(is_polar, exchange_and_filter, lambda inner: inner, flattened)
        fields_now = fields_now + time_step * filtered.reshape(fields_now.shape)
    return fields_now


def solution(mesh):
    return jax.shard_map(
        local,
        mesh=mesh,
        in_specs=(P(None, None, "lon", "lat"), P(None, "lat"), P(None, "lat"), P(), P()),
        out_specs=P(None, None, "lon", "lat"),
        check_vma=False,
    )
```

```python
import math

import jax
import jax.numpy as jnp
from jax import lax
from jax.sharding import PartitionSpec as P

ITERS = 3


time_step = 0.15
highest = lax.Precision.HIGHEST


def with_halo(block, sides, width, periodic):
    for axis, dim in sides:
        count = lax.axis_size(axis)
        forward = [(i, i + 1) for i in range(count - 1)]
        if periodic:
            forward.append((count - 1, 0))
        backward = [(target, source) for source, target in forward]
        low = lax.ppermute(
            lax.slice_in_dim(block, block.shape[dim] - width, None, axis=dim), axis, forward
        )
        high = lax.ppermute(lax.slice_in_dim(block, 0, width, axis=dim), axis, backward)
        block = jnp.concatenate([low, block, high], axis=dim)
    return block


def latitude(row_ids, lat_total):
    return (row_ids.astype(jnp.float32) + 0.5) * (math.pi / lat_total) - 0.5 * math.pi


def damping(row_ids, lat_total, circle_len):
    cos_ratio = jnp.cos(latitude(row_ids, lat_total)) / math.cos(0.25 * math.pi)
    wave_ids = jnp.arange(circle_len // 2 + 1)
    sine_vals = jnp.sin(wave_ids.astype(jnp.float32) * (math.pi / circle_len))
    safe_sines = jnp.where(wave_ids == 0, 1.0, sine_vals)
    return jnp.where(
        wave_ids[None, :] == 0, 1.0, jnp.minimum(1.0, cos_ratio[:, None] / safe_sines[None, :])
    )


def tendency(
    fields_now,
    north_rows,
    south_rows,
    east_cols,
    west_cols,
    row_ids,
    lat_total,
    wind_zonal,
    wind_merid,
    layer_depth,
    diffusion,
):
    latitudes = latitude(row_ids, lat_total)
    cos_centre = jnp.cos(latitudes)
    cos_north = jnp.cos(latitude(row_ids + 1, lat_total))
    cos_south = jnp.cos(latitude(row_ids - 1, lat_total))
    coriolis = jnp.sin(latitudes)
    zonal_diff = (east_cols - west_cols) / (2.0 * cos_centre)
    merid_diff = 0.5 * (north_rows - south_rows)
    advect = wind_zonal[:, None, :] * zonal_diff + wind_merid[:, None, :] * merid_diff
    diverge = zonal_diff[0] + (north_rows[1] * cos_north - south_rows[1] * cos_south) / (
        2.0 * cos_centre
    )
    zonal_tend = -advect[0] + coriolis * fields_now[1] - zonal_diff[2]
    merid_tend = -advect[1] - coriolis * fields_now[0] - merid_diff[2]
    height_tend = -advect[2] - layer_depth[:, None, None] * diverge
    tracer_tend = -advect[3:] + diffusion[:, :, None, None] * (
        north_rows[3:] - 2.0 * fields_now[3:] + south_rows[3:]
    )
    return jnp.concatenate(
        [zonal_tend[None], merid_tend[None], height_tend[None], tracer_tend], axis=0
    )


def trig_pair(rows, cols, length, sign):
    phases = (
        jnp.arange(rows, dtype=jnp.int32)[:, None] * jnp.arange(cols, dtype=jnp.int32)[None, :]
    ) % length
    angles = phases.astype(jnp.float32) * (2.0 * math.pi / length)
    return jnp.cos(angles), sign * jnp.sin(angles)


def mm(table, data, spec):
    return jnp.einsum(spec, table, data, precision=highest)


def filter_circles(sector, factors, devs, local, lon_pos):
    total = devs * local
    offsets = jnp.arange(devs, dtype=jnp.int32)
    source = (lon_pos - offsets) % devs
    dest = (lon_pos + offsets) % devs
    c16, s16 = trig_pair(devs, devs, devs, -1.0)
    src_c = jnp.take(c16, source, axis=1)
    src_s = jnp.take(s16, source, axis=1)
    dst_c = jnp.take(c16, dest, axis=0)
    dst_s = jnp.take(s16, dest, axis=0)
    cm, sm = trig_pair(local, local, local, -1.0)
    tw_c, tw_s = trig_pair(devs, local, total, -1.0)
    tw_c = tw_c[:, :, None]
    tw_s = tw_s[:, :, None]
    a_re = mm(src_c, sector, "ks,smc->kmc")
    a_im = mm(src_s, sector, "ks,smc->kmc")
    b_re = a_re * tw_c - a_im * tw_s
    b_im = a_re * tw_s + a_im * tw_c
    x_re = mm(cm, b_re, "qm,kmc->kqc") - mm(sm, b_im, "qm,kmc->kqc")
    x_im = mm(cm, b_im, "qm,kmc->kqc") + mm(sm, b_re, "qm,kmc->kqc")
    y_re = x_re * factors
    y_im = x_im * factors
    d_re = mm(cm, y_re, "mq,kqc->kmc") + mm(sm, y_im, "mq,kqc->kmc")
    d_im = mm(cm, y_im, "mq,kqc->kmc") - mm(sm, y_re, "mq,kqc->kmc")
    e_re = d_re * tw_c + d_im * tw_s
    e_im = d_im * tw_c - d_re * tw_s
    out = mm(dst_c, e_re, "sk,kmc->smc") + mm(dst_s, e_im, "sk,kmc->smc")
    return out * (1.0 / total)


def rotate(slabs, lat_axis, lon_axis, active):
    count = lax.axis_size(lon_axis)
    parts = [slabs[0]]
    for offset in range(1, count):
        pairs = [
            (row * count + i, row * count + (i + offset) % count)
            for row in active
            for i in range(count)
        ]
        parts.append(lax.ppermute(slabs[offset], (lat_axis, lon_axis), pairs))
    return jnp.stack(parts, axis=0)


def local(prognostic, wind_zonal, wind_merid, layer_depth, diffusion):
    field_count, level_count, col_count, row_count = prognostic.shape
    lat_devs = lax.axis_size("lat")
    lon_devs = lax.axis_size("lon")
    lat_total = row_count * lat_devs
    circle_len = col_count * lon_devs
    lat_pos = lax.axis_index("lat")
    lon_pos = lax.axis_index("lon")
    row_ids = lat_pos * row_count + jnp.arange(row_count, dtype=jnp.int32)
    quarter = lat_devs // 4
    is_polar = (lat_pos < quarter) | (lat_pos >= lat_devs - quarter)
    vectors = field_count * level_count
    slab_rows = row_count // lon_devs
    circles = vectors * slab_rows

    start_row = lat_pos * row_count + lon_pos * slab_rows
    halfway = damping(start_row + jnp.arange(slab_rows, dtype=jnp.int32), lat_total, circle_len)
    mirrored = halfway[:, 1 : circle_len // 2][:, ::-1]
    full = jnp.concatenate([halfway, mirrored], axis=1)
    by_k = full.reshape(slab_rows, col_count, lon_devs)
    by_k = jnp.transpose(by_k, (2, 1, 0))
    factors = jnp.broadcast_to(
        by_k[:, :, None, :], (lon_devs, col_count, vectors, slab_rows)
    ).reshape(lon_devs, col_count, circles)

    polar_rows = [i for i in range(lat_devs) if i < quarter or i >= lat_devs - quarter]
    offsets = jnp.arange(lon_devs, dtype=jnp.int32)

    def exchange_and_filter(flat):
        send = flat.reshape(vectors, col_count, lon_devs, slab_rows)
        send = jnp.transpose(send, (2, 1, 0, 3)).reshape(lon_devs, col_count, circles)
        send = jnp.take(send, (lon_pos + offsets) % lon_devs, axis=0)
        recv = rotate(send, "lat", "lon", polar_rows)
        smoothed = lax.cond(
            is_polar,
            lambda inner: filter_circles(inner, factors, lon_devs, col_count, lon_pos),
            lambda inner: inner,
            recv,
        )
        back = rotate(smoothed, "lat", "lon", polar_rows)

        def unpack(slabs):
            slabs = jnp.take(slabs, (lon_pos - offsets) % lon_devs, axis=0)
            slabs = slabs.reshape(lon_devs, col_count, vectors, slab_rows)
            return jnp.transpose(slabs, (2, 1, 0, 3)).reshape(vectors, col_count, row_count)

        return lax.cond(is_polar, unpack, lambda inner: flat, back)

    fields_now = prognostic
    for substep in range(ITERS):
        lat_padded = with_halo(fields_now, (("lat", 3),), 1, False)
        lon_padded = with_halo(fields_now, (("lon", 2),), 1, True)
        tendency_now = tendency(
            fields_now,
            lat_padded[:, :, :, 2:],
            lat_padded[:, :, :, :-2],
            lon_padded[:, :, 2:],
            lon_padded[:, :, :-2],
            row_ids,
            lat_total,
            wind_zonal,
            wind_merid,
            layer_depth,
            diffusion,
        )
        flattened = tendency_now.reshape(vectors, col_count, row_count)
        filtered = exchange_and_filter(flattened)
        fields_now = fields_now + time_step * filtered.reshape(fields_now.shape)
    return fields_now


def solution(mesh):
    return jax.shard_map(
        local,
        mesh=mesh,
        in_specs=(P(None, None, "lon", "lat"), P(None, "lat"), P(None, "lat"), P(), P()),
        out_specs=P(None, None, "lon", "lat"),
        check_vma=False,
    )
```

```python
import math

import jax
import jax.numpy as jnp
from jax import lax
from jax.sharding import PartitionSpec as P

ITERS = 3


time_step = 0.15
highest = lax.Precision.HIGH


def with_halo(block, sides, width, periodic):
    for axis, dim in sides:
        count = lax.axis_size(axis)
        forward = [(i, i + 1) for i in range(count - 1)]
        if periodic:
            forward.append((count - 1, 0))
        backward = [(target, source) for source, target in forward]
        low = lax.ppermute(
            lax.slice_in_dim(block, block.shape[dim] - width, None, axis=dim), axis, forward
        )
        high = lax.ppermute(lax.slice_in_dim(block, 0, width, axis=dim), axis, backward)
        block = jnp.concatenate([low, block, high], axis=dim)
    return block


def latitude(row_ids, lat_total):
    return (row_ids.astype(jnp.float32) + 0.5) * (math.pi / lat_total) - 0.5 * math.pi


def damping(row_ids, lat_total, circle_len):
    cos_ratio = jnp.cos(latitude(row_ids, lat_total)) / math.cos(0.25 * math.pi)
    wave_ids = jnp.arange(circle_len // 2 + 1)
    sine_vals = jnp.sin(wave_ids.astype(jnp.float32) * (math.pi / circle_len))
    safe_sines = jnp.where(wave_ids == 0, 1.0, sine_vals)
    return jnp.where(
        wave_ids[None, :] == 0, 1.0, jnp.minimum(1.0, cos_ratio[:, None] / safe_sines[None, :])
    )


def tendency(
    fields_now,
    north_rows,
    south_rows,
    east_cols,
    west_cols,
    row_ids,
    lat_total,
    wind_zonal,
    wind_merid,
    layer_depth,
    diffusion,
):
    latitudes = latitude(row_ids, lat_total)
    cos_centre = jnp.cos(latitudes)
    cos_north = jnp.cos(latitude(row_ids + 1, lat_total))
    cos_south = jnp.cos(latitude(row_ids - 1, lat_total))
    coriolis = jnp.sin(latitudes)
    zonal_diff = (east_cols - west_cols) / (2.0 * cos_centre)
    merid_diff = 0.5 * (north_rows - south_rows)
    advect = wind_zonal[:, None, :] * zonal_diff + wind_merid[:, None, :] * merid_diff
    diverge = zonal_diff[0] + (north_rows[1] * cos_north - south_rows[1] * cos_south) / (
        2.0 * cos_centre
    )
    zonal_tend = -advect[0] + coriolis * fields_now[1] - zonal_diff[2]
    merid_tend = -advect[1] - coriolis * fields_now[0] - merid_diff[2]
    height_tend = -advect[2] - layer_depth[:, None, None] * diverge
    tracer_tend = -advect[3:] + diffusion[:, :, None, None] * (
        north_rows[3:] - 2.0 * fields_now[3:] + south_rows[3:]
    )
    return jnp.concatenate(
        [zonal_tend[None], merid_tend[None], height_tend[None], tracer_tend], axis=0
    )


def trig_pair(rows, cols, length, sign):
    phases = (
        jnp.arange(rows, dtype=jnp.int32)[:, None] * jnp.arange(cols, dtype=jnp.int32)[None, :]
    ) % length
    angles = phases.astype(jnp.float32) * (2.0 * math.pi / length)
    return jnp.cos(angles), sign * jnp.sin(angles)


def mm(table, data, spec):
    return jnp.einsum(spec, table, data, precision=highest)


def filter_circles(sector, factors, devs, local):
    total = devs * local
    c16, s16 = trig_pair(devs, devs, devs, -1.0)
    cm, sm = trig_pair(local, local, local, -1.0)
    tw_c, tw_s = trig_pair(devs, local, total, -1.0)
    tw_c = tw_c[:, :, None]
    tw_s = tw_s[:, :, None]
    a_re = mm(c16, sector, "ks,smc->kmc")
    a_im = mm(s16, sector, "ks,smc->kmc")
    b_re = a_re * tw_c - a_im * tw_s
    b_im = a_re * tw_s + a_im * tw_c
    x_re = mm(cm, b_re, "qm,kmc->kqc") - mm(sm, b_im, "qm,kmc->kqc")
    x_im = mm(cm, b_im, "qm,kmc->kqc") + mm(sm, b_re, "qm,kmc->kqc")
    y_re = x_re * factors
    y_im = x_im * factors
    d_re = mm(cm, y_re, "mq,kqc->kmc") + mm(sm, y_im, "mq,kqc->kmc")
    d_im = mm(cm, y_im, "mq,kqc->kmc") - mm(sm, y_re, "mq,kqc->kmc")
    e_re = d_re * tw_c + d_im * tw_s
    e_im = d_im * tw_c - d_re * tw_s
    out = mm(c16, e_re, "sk,kmc->smc") + mm(s16, e_im, "sk,kmc->smc")
    return out * (1.0 / total)


def local(prognostic, wind_zonal, wind_merid, layer_depth, diffusion):
    field_count, level_count, col_count, row_count = prognostic.shape
    lat_devs = lax.axis_size("lat")
    lon_devs = lax.axis_size("lon")
    lat_total = row_count * lat_devs
    circle_len = col_count * lon_devs
    lat_pos = lax.axis_index("lat")
    lon_pos = lax.axis_index("lon")
    row_ids = lat_pos * row_count + jnp.arange(row_count, dtype=jnp.int32)
    quarter = lat_devs // 4
    is_polar = (lat_pos < quarter) | (lat_pos >= lat_devs - quarter)
    vectors = field_count * level_count
    slab_rows = row_count // lon_devs
    circles = vectors * slab_rows

    start_row = lat_pos * row_count + lon_pos * slab_rows
    halfway = damping(start_row + jnp.arange(slab_rows, dtype=jnp.int32), lat_total, circle_len)
    mirrored = halfway[:, 1 : circle_len // 2][:, ::-1]
    full = jnp.concatenate([halfway, mirrored], axis=1)
    by_k = full.reshape(slab_rows, col_count, lon_devs)
    by_k = jnp.transpose(by_k, (2, 1, 0))
    factors = jnp.broadcast_to(
        by_k[:, :, None, :], (lon_devs, col_count, vectors, slab_rows)
    ).reshape(lon_devs, col_count, circles)

    def exchange_and_filter(flat):
        send = flat.reshape(vectors, col_count, lon_devs, slab_rows)
        send = jnp.transpose(send, (2, 1, 0, 3)).reshape(lon_devs, col_count, circles)
        recv = lax.all_to_all(send, "lon", 0, 0, tiled=True)
        smoothed = filter_circles(recv, factors, lon_devs, col_count)
        back = lax.all_to_all(smoothed, "lon", 0, 0, tiled=True)
        back = back.reshape(lon_devs, col_count, vectors, slab_rows)
        return jnp.transpose(back, (2, 1, 0, 3)).reshape(vectors, col_count, row_count)

    fields_now = prognostic
    for substep in range(ITERS):
        lat_padded = with_halo(fields_now, (("lat", 3),), 1, False)
        lon_padded = with_halo(fields_now, (("lon", 2),), 1, True)
        tendency_now = tendency(
            fields_now,
            lat_padded[:, :, :, 2:],
            lat_padded[:, :, :, :-2],
            lon_padded[:, :, 2:],
            lon_padded[:, :, :-2],
            row_ids,
            lat_total,
            wind_zonal,
            wind_merid,
            layer_depth,
            diffusion,
        )
        flattened = tendency_now.reshape(vectors, col_count, row_count)
        filtered = lax.cond(is_polar, exchange_and_filter, lambda inner: inner, flattened)
        fields_now = fields_now + time_step * filtered.reshape(fields_now.shape)
    return fields_now


def solution(mesh):
    return jax.shard_map(
        local,
        mesh=mesh,
        in_specs=(P(None, None, "lon", "lat"), P(None, "lat"), P(None, "lat"), P(), P()),
        out_specs=P(None, None, "lon", "lat"),
        check_vma=False,
    )
```

```python
import math

import jax
import jax.numpy as jnp
from jax import lax
from jax.sharding import PartitionSpec as P

ITERS = 3


time_step = 0.15
highest = lax.Precision.HIGH


def with_halo(block, sides, width, periodic):
    for axis, dim in sides:
        count = lax.axis_size(axis)
        forward = [(i, i + 1) for i in range(count - 1)]
        if periodic:
            forward.append((count - 1, 0))
        backward = [(target, source) for source, target in forward]
        low = lax.ppermute(
            lax.slice_in_dim(block, block.shape[dim] - width, None, axis=dim), axis, forward
        )
        high = lax.ppermute(lax.slice_in_dim(block, 0, width, axis=dim), axis, backward)
        block = jnp.concatenate([low, block, high], axis=dim)
    return block


def latitude(row_ids, lat_total):
    return (row_ids.astype(jnp.float32) + 0.5) * (math.pi / lat_total) - 0.5 * math.pi


def damping(row_ids, lat_total, circle_len):
    cos_ratio = jnp.cos(latitude(row_ids, lat_total)) / math.cos(0.25 * math.pi)
    wave_ids = jnp.arange(circle_len // 2 + 1)
    sine_vals = jnp.sin(wave_ids.astype(jnp.float32) * (math.pi / circle_len))
    safe_sines = jnp.where(wave_ids == 0, 1.0, sine_vals)
    return jnp.where(
        wave_ids[None, :] == 0, 1.0, jnp.minimum(1.0, cos_ratio[:, None] / safe_sines[None, :])
    )


def tendency(
    fields_now,
    north_rows,
    south_rows,
    east_cols,
    west_cols,
    row_ids,
    lat_total,
    wind_zonal,
    wind_merid,
    layer_depth,
    diffusion,
):
    latitudes = latitude(row_ids, lat_total)
    cos_centre = jnp.cos(latitudes)
    cos_north = jnp.cos(latitude(row_ids + 1, lat_total))
    cos_south = jnp.cos(latitude(row_ids - 1, lat_total))
    coriolis = jnp.sin(latitudes)
    zonal_diff = (east_cols - west_cols) / (2.0 * cos_centre)
    merid_diff = 0.5 * (north_rows - south_rows)
    advect = wind_zonal[:, None, :] * zonal_diff + wind_merid[:, None, :] * merid_diff
    diverge = zonal_diff[0] + (north_rows[1] * cos_north - south_rows[1] * cos_south) / (
        2.0 * cos_centre
    )
    zonal_tend = -advect[0] + coriolis * fields_now[1] - zonal_diff[2]
    merid_tend = -advect[1] - coriolis * fields_now[0] - merid_diff[2]
    height_tend = -advect[2] - layer_depth[:, None, None] * diverge
    tracer_tend = -advect[3:] + diffusion[:, :, None, None] * (
        north_rows[3:] - 2.0 * fields_now[3:] + south_rows[3:]
    )
    return jnp.concatenate(
        [zonal_tend[None], merid_tend[None], height_tend[None], tracer_tend], axis=0
    )


def trig_pair(rows, cols, length, sign):
    phases = (
        jnp.arange(rows, dtype=jnp.int32)[:, None] * jnp.arange(cols, dtype=jnp.int32)[None, :]
    ) % length
    angles = phases.astype(jnp.float32) * (2.0 * math.pi / length)
    return jnp.cos(angles), sign * jnp.sin(angles)


def mm(table, data, spec):
    return jnp.einsum(spec, table, data, precision=highest)


def filter_circles(sector, factors, devs, local):
    total = devs * local
    c16, s16 = trig_pair(devs, devs, devs, -1.0)
    cm, sm = trig_pair(local, local, local, -1.0)
    tw_c, tw_s = trig_pair(devs, local, total, -1.0)
    tw_c = tw_c[:, :, None]
    tw_s = tw_s[:, :, None]
    a_re = mm(c16, sector, "ks,smc->kmc")
    a_im = mm(s16, sector, "ks,smc->kmc")
    b_re = a_re * tw_c - a_im * tw_s
    b_im = a_re * tw_s + a_im * tw_c
    x_re = mm(cm, b_re, "qm,kmc->kqc") - mm(sm, b_im, "qm,kmc->kqc")
    x_im = mm(cm, b_im, "qm,kmc->kqc") + mm(sm, b_re, "qm,kmc->kqc")
    y_re = x_re * factors
    y_im = x_im * factors
    d_re = mm(cm, y_re, "mq,kqc->kmc") + mm(sm, y_im, "mq,kqc->kmc")
    d_im = mm(cm, y_im, "mq,kqc->kmc") - mm(sm, y_re, "mq,kqc->kmc")
    e_re = d_re * tw_c + d_im * tw_s
    e_im = d_im * tw_c - d_re * tw_s
    out = mm(c16, e_re, "sk,kmc->smc") + mm(s16, e_im, "sk,kmc->smc")
    return out * (1.0 / total)


def local(prognostic, wind_zonal, wind_merid, layer_depth, diffusion):
    field_count, level_count, col_count, row_count = prognostic.shape
    lat_devs = lax.axis_size("lat")
    lon_devs = lax.axis_size("lon")
    lat_total = row_count * lat_devs
    circle_len = col_count * lon_devs
    lat_pos = lax.axis_index("lat")
    lon_pos = lax.axis_index("lon")
    row_ids = lat_pos * row_count + jnp.arange(row_count, dtype=jnp.int32)
    quarter = lat_devs // 4
    is_polar = (lat_pos < quarter) | (lat_pos >= lat_devs - quarter)
    vectors = field_count * level_count
    slab_rows = row_count // lon_devs
    circles = vectors * slab_rows

    start_row = lat_pos * row_count + lon_pos * slab_rows
    halfway = damping(start_row + jnp.arange(slab_rows, dtype=jnp.int32), lat_total, circle_len)
    mirrored = halfway[:, 1 : circle_len // 2][:, ::-1]
    full = jnp.concatenate([halfway, mirrored], axis=1)
    by_k = full.reshape(slab_rows, col_count, lon_devs)
    by_k = jnp.transpose(by_k, (2, 1, 0))
    factors = jnp.broadcast_to(
        by_k[:, :, None, :], (lon_devs, col_count, vectors, slab_rows)
    ).reshape(lon_devs, col_count, circles)

    inner = lon_devs // 2 if lon_devs % 2 == 0 else lon_devs
    outer = lon_devs // inner
    first_groups = [[inner * a + b for b in range(inner)] for a in range(outer)]
    second_groups = [[inner * a + b for a in range(outer)] for b in range(inner)]

    def two_stage(slabs):
        rest = slabs.shape[2:]
        moved = lax.all_to_all(slabs, "lon", 0, 0, tiled=True, axis_index_groups=first_groups)
        moved = jnp.swapaxes(moved, 0, 1)
        moved = lax.all_to_all(moved, "lon", 0, 0, tiled=True, axis_index_groups=second_groups)
        return moved.reshape((lon_devs,) + rest)

    def exchange_and_filter(flat):
        send = flat.reshape(vectors, col_count, outer, inner, slab_rows)
        send = jnp.transpose(send, (3, 2, 1, 0, 4)).reshape(inner, outer, col_count, circles)
        recv = two_stage(send)
        smoothed = filter_circles(recv, factors, lon_devs, col_count)
        smoothed = jnp.swapaxes(smoothed.reshape(outer, inner, col_count, circles), 0, 1)
        back = two_stage(smoothed)
        back = back.reshape(lon_devs, col_count, vectors, slab_rows)
        return jnp.transpose(back, (2, 1, 0, 3)).reshape(vectors, col_count, row_count)

    fields_now = prognostic
    for substep in range(ITERS):
        lat_padded = with_halo(fields_now, (("lat", 3),), 1, False)
        lon_padded = with_halo(fields_now, (("lon", 2),), 1, True)
        tendency_now = tendency(
            fields_now,
            lat_padded[:, :, :, 2:],
            lat_padded[:, :, :, :-2],
            lon_padded[:, :, 2:],
            lon_padded[:, :, :-2],
            row_ids,
            lat_total,
            wind_zonal,
            wind_merid,
            layer_depth,
            diffusion,
        )
        flattened = tendency_now.reshape(vectors, col_count, row_count)
        filtered = lax.cond(is_polar, exchange_and_filter, lambda inner: inner, flattened)
        fields_now = fields_now + time_step * filtered.reshape(fields_now.shape)
    return fields_now


def solution(mesh):
    return jax.shard_map(
        local,
        mesh=mesh,
        in_specs=(P(None, None, "lon", "lat"), P(None, "lat"), P(None, "lat"), P(), P()),
        out_specs=P(None, None, "lon", "lat"),
        check_vma=False,
    )
```

```python
import math

import jax
import jax.numpy as jnp
from jax import lax
from jax.sharding import PartitionSpec as P

ITERS = 3


time_step = 0.15
precision = lax.Precision.HIGH


def latitude(row_ids, lat_total):
    return (row_ids.astype(jnp.float32) + 0.5) * (math.pi / lat_total) - 0.5 * math.pi


def damping(row_ids, lat_total, circle_len):
    cos_ratio = jnp.cos(latitude(row_ids, lat_total)) / math.cos(0.25 * math.pi)
    wave_ids = jnp.arange(circle_len // 2 + 1)
    sine_vals = jnp.sin(wave_ids.astype(jnp.float32) * (math.pi / circle_len))
    safe_sines = jnp.where(wave_ids == 0, 1.0, sine_vals)
    return jnp.where(
        wave_ids[None, :] == 0, 1.0, jnp.minimum(1.0, cos_ratio[:, None] / safe_sines[None, :])
    )


def tendency(fields_now, north_rows, south_rows, row_ids, lat_total, winds_u, winds_v, depth, diffusion):
    latitudes = latitude(row_ids, lat_total)[:, None]
    cos_centre = jnp.cos(latitudes)
    cos_north = jnp.cos(latitude(row_ids + 1, lat_total))[:, None]
    cos_south = jnp.cos(latitude(row_ids - 1, lat_total))[:, None]
    coriolis = jnp.sin(latitudes)
    east_cols = jnp.roll(fields_now, -1, axis=3)
    west_cols = jnp.roll(fields_now, 1, axis=3)
    zonal_diff = (east_cols - west_cols) / (2.0 * cos_centre)
    merid_diff = 0.5 * (north_rows - south_rows)
    advect = winds_u[:, :, None] * zonal_diff + winds_v[:, :, None] * merid_diff
    diverge = zonal_diff[0] + (north_rows[1] * cos_north - south_rows[1] * cos_south) / (
        2.0 * cos_centre
    )
    zonal_tend = -advect[0] + coriolis * fields_now[1] - zonal_diff[2]
    merid_tend = -advect[1] - coriolis * fields_now[0] - merid_diff[2]
    height_tend = -advect[2] - depth[:, None, None] * diverge
    tracer_tend = -advect[3:] + diffusion[:, :, None, None] * (
        north_rows[3:] - 2.0 * fields_now[3:] + south_rows[3:]
    )
    return jnp.concatenate(
        [zonal_tend[None], merid_tend[None], height_tend[None], tracer_tend], axis=0
    )


def trig_pair(rows, cols, length):
    phases = (
        jnp.arange(rows, dtype=jnp.int32)[:, None] * jnp.arange(cols, dtype=jnp.int32)[None, :]
    ) % length
    angles = phases.astype(jnp.float32) * (2.0 * math.pi / length)
    return jnp.cos(angles), jnp.sin(angles)


def mm(spec, left, right):
    return jnp.einsum(spec, left, right, precision=precision)


def split_length(total):
    lanes = 128
    return total // lanes, lanes


def filter_rows(circles, factors):
    count, total = circles.shape
    outer, lanes = split_length(total)
    c_o, s_o = trig_pair(outer, outer, outer)
    c_l, s_l = trig_pair(lanes, lanes, lanes)
    tw_c, tw_s = trig_pair(outer, lanes, total)
    tw_c = tw_c[:, None, :]
    tw_s = tw_s[:, None, :]
    first = jnp.concatenate([c_o, -s_o], axis=0)
    last = jnp.concatenate([c_o, -s_o], axis=1) * (1.0 / total)
    fwd = jnp.concatenate(
        [jnp.concatenate([c_l, -s_l], axis=1), jnp.concatenate([s_l, c_l], axis=1)], axis=0
    )
    inv = jnp.concatenate(
        [jnp.concatenate([c_l, s_l], axis=1), jnp.concatenate([-s_l, c_l], axis=1)], axis=0
    )
    grid = jnp.transpose(circles.reshape(count, outer, lanes), (1, 0, 2))
    spread = mm("ka,af->kf", first, grid.reshape(outer, count * lanes))
    spread = spread.reshape(2, outer, count, lanes)
    b_re = spread[0] * tw_c + spread[1] * tw_s
    b_im = spread[1] * tw_c - spread[0] * tw_s
    joined = jnp.concatenate([b_re, b_im], axis=2)
    spectrum = mm("kcb,bq->kcq", joined, fwd) * factors
    back = mm("kcq,qb->kcb", spectrum, inv)
    d_re = back[:, :, :lanes]
    d_im = back[:, :, lanes:]
    e_re = d_re * tw_c - d_im * tw_s
    e_im = d_im * tw_c + d_re * tw_s
    stacked = jnp.concatenate([e_re, e_im], axis=0).reshape(2 * outer, count * lanes)
    rows = mm("ak,kf->af", last, stacked).reshape(outer, count, lanes)
    return jnp.transpose(rows, (1, 0, 2)).reshape(count, total)


def local(prognostic, wind_zonal, wind_merid, layer_depth, diffusion):
    field_count, level_count, col_count, row_count = prognostic.shape
    lat_devs = lax.axis_size("lat")
    lon_devs = lax.axis_size("lon")
    lat_total = row_count * lat_devs
    circle_len = col_count * lon_devs
    lat_pos = lax.axis_index("lat")
    lon_pos = lax.axis_index("lon")
    quarter = lat_devs // 4
    is_polar = (lat_pos < quarter) | (lat_pos >= lat_devs - quarter)
    vectors = field_count * level_count
    slab_rows = row_count // lon_devs
    devices = lat_devs * lon_devs
    row_ids = lat_pos * row_count + lon_pos * slab_rows + jnp.arange(slab_rows, dtype=jnp.int32)
    winds_u = lax.dynamic_slice_in_dim(wind_zonal, lon_pos * slab_rows, slab_rows, axis=1)
    winds_v = lax.dynamic_slice_in_dim(wind_merid, lon_pos * slab_rows, slab_rows, axis=1)

    outer, lanes = split_length(circle_len)
    halfway = damping(row_ids, lat_total, circle_len)
    mirrored = halfway[:, 1 : circle_len // 2][:, ::-1]
    full = jnp.concatenate([halfway, mirrored], axis=1)
    by_k = jnp.transpose(full.reshape(slab_rows, lanes, outer), (2, 0, 1))
    by_k = jnp.broadcast_to(by_k[:, None], (outer, vectors, slab_rows, lanes))
    by_k = by_k.reshape(outer, vectors * slab_rows, lanes)
    factors = jnp.concatenate([by_k, by_k], axis=2)

    send = prognostic.reshape(vectors, col_count, lon_devs, slab_rows)
    send = jnp.transpose(send, (2, 1, 0, 3))
    recv = lax.all_to_all(send, "lon", 0, 0, tiled=True)
    state = jnp.transpose(recv, (2, 3, 0, 1)).reshape(
        field_count, level_count, slab_rows, circle_len
    )

    up = [(q, q + 1) for q in range(devices - 1)]
    down = [(q + 1, q) for q in range(devices - 1)]
    for substep in range(ITERS):
        rows = state.reshape(vectors, slab_rows, circle_len)
        south = lax.ppermute(rows[:, -1, :], ("lat", "lon"), up)
        north = lax.ppermute(rows[:, 0, :], ("lat", "lon"), down)
        north_rows = jnp.concatenate([rows[:, 1:], north[:, None]], axis=1)
        south_rows = jnp.concatenate([south[:, None], rows[:, :-1]], axis=1)
        shape = state.shape
        tendency_now = tendency(
            state,
            north_rows.reshape(shape),
            south_rows.reshape(shape),
            row_ids,
            lat_total,
            winds_u,
            winds_v,
            layer_depth,
            diffusion,
        )
        flat = tendency_now.reshape(vectors * slab_rows, circle_len)
        filtered = lax.cond(
            is_polar, lambda inner: filter_rows(inner, factors), lambda inner: inner, flat
        )
        state = state + time_step * filtered.reshape(shape)

    out = state.reshape(vectors, slab_rows, lon_devs, col_count)
    out = jnp.transpose(out, (2, 3, 0, 1))
    out = lax.all_to_all(out, "lon", 0, 0, tiled=True)
    out = jnp.transpose(out, (2, 1, 0, 3)).reshape(prognostic.shape)
    return out


def solution(mesh):
    return jax.shard_map(
        local,
        mesh=mesh,
        in_specs=(P(None, None, "lon", "lat"), P(None, "lat"), P(None, "lat"), P(), P()),
        out_specs=P(None, None, "lon", "lat"),
        check_vma=False,
    )
```

```python
import math

import jax
import jax.numpy as jnp
from jax import lax
from jax.sharding import PartitionSpec as P

ITERS = 3


time_step = 0.15
precision = lax.Precision.HIGH


def latitude(row_ids, lat_total):
    return (row_ids.astype(jnp.float32) + 0.5) * (math.pi / lat_total) - 0.5 * math.pi


def damping(row_ids, lat_total, circle_len):
    cos_ratio = jnp.cos(latitude(row_ids, lat_total)) / math.cos(0.25 * math.pi)
    wave_ids = jnp.arange(circle_len // 2 + 1)
    sine_vals = jnp.sin(wave_ids.astype(jnp.float32) * (math.pi / circle_len))
    safe_sines = jnp.where(wave_ids == 0, 1.0, sine_vals)
    return jnp.where(
        wave_ids[None, :] == 0, 1.0, jnp.minimum(1.0, cos_ratio[:, None] / safe_sines[None, :])
    )


def tendency(rows, north_rows, south_rows, row_ids, lat_total, winds_u, winds_v, depth, diffusion):
    levels = depth.shape[0]
    fields = rows.shape[0] // levels
    latitudes = latitude(row_ids, lat_total)[:, None]
    cos_centre = jnp.cos(latitudes)
    cos_north = jnp.cos(latitude(row_ids + 1, lat_total))[:, None]
    cos_south = jnp.cos(latitude(row_ids - 1, lat_total))[:, None]
    coriolis = jnp.sin(latitudes)
    wind_u = jnp.tile(winds_u, (fields, 1))[:, :, None]
    wind_v = jnp.tile(winds_v, (fields, 1))[:, :, None]
    east_cols = jnp.roll(rows, -1, axis=2)
    west_cols = jnp.roll(rows, 1, axis=2)
    zonal_diff = (east_cols - west_cols) / (2.0 * cos_centre)
    merid_diff = 0.5 * (north_rows - south_rows)
    advect = wind_u * zonal_diff + wind_v * merid_diff
    u_part = slice(0, levels)
    v_part = slice(levels, 2 * levels)
    h_part = slice(2 * levels, 3 * levels)
    t_part = slice(3 * levels, None)
    diverge = zonal_diff[u_part] + (
        north_rows[v_part] * cos_north - south_rows[v_part] * cos_south
    ) / (2.0 * cos_centre)
    zonal_tend = -advect[u_part] + coriolis * rows[v_part] - zonal_diff[h_part]
    merid_tend = -advect[v_part] - coriolis * rows[u_part] - merid_diff[h_part]
    height_tend = -advect[h_part] - depth[:, None, None] * diverge
    tracer_tend = -advect[t_part] + diffusion.reshape(-1)[:, None, None] * (
        north_rows[t_part] - 2.0 * rows[t_part] + south_rows[t_part]
    )
    return jnp.concatenate([zonal_tend, merid_tend, height_tend, tracer_tend], axis=0)


def trig_pair(rows, cols, length):
    phases = (
        jnp.arange(rows, dtype=jnp.int32)[:, None] * jnp.arange(cols, dtype=jnp.int32)[None, :]
    ) % length
    angles = phases.astype(jnp.float32) * (2.0 * math.pi / length)
    return jnp.cos(angles), jnp.sin(angles)


def mm(spec, left, right):
    return jnp.einsum(spec, left, right, precision=precision)


def split_length(total):
    lanes = 128
    return total // lanes, lanes


def filter_rows(circles, factors):
    count, total = circles.shape
    outer, lanes = split_length(total)
    c_o, s_o = trig_pair(outer, outer, outer)
    c_l, s_l = trig_pair(lanes, lanes, lanes)
    tw_c, tw_s = trig_pair(outer, lanes, total)
    tw_c = tw_c[:, None, :]
    tw_s = tw_s[:, None, :]
    first = jnp.concatenate([c_o, -s_o], axis=0)
    last = jnp.concatenate([c_o, -s_o], axis=1) * (1.0 / total)
    fwd = jnp.concatenate(
        [jnp.concatenate([c_l, -s_l], axis=1), jnp.concatenate([s_l, c_l], axis=1)], axis=0
    )
    inv = jnp.concatenate(
        [jnp.concatenate([c_l, s_l], axis=1), jnp.concatenate([-s_l, c_l], axis=1)], axis=0
    )
    grid = jnp.transpose(circles.reshape(count, outer, lanes), (1, 0, 2))
    spread = mm("ka,af->kf", first, grid.reshape(outer, count * lanes))
    spread = spread.reshape(2, outer, count, lanes)
    b_re = spread[0] * tw_c + spread[1] * tw_s
    b_im = spread[1] * tw_c - spread[0] * tw_s
    joined = jnp.concatenate([b_re, b_im], axis=2)
    spectrum = mm("kcb,bq->kcq", joined, fwd) * factors
    back = mm("kcq,qb->kcb", spectrum, inv)
    d_re = back[:, :, :lanes]
    d_im = back[:, :, lanes:]
    e_re = d_re * tw_c - d_im * tw_s
    e_im = d_im * tw_c + d_re * tw_s
    stacked = jnp.concatenate([e_re, e_im], axis=0).reshape(2 * outer, count * lanes)
    rows = mm("ak,kf->af", last, stacked).reshape(outer, count, lanes)
    return jnp.transpose(rows, (1, 0, 2)).reshape(count, total)


def local(prognostic, wind_zonal, wind_merid, layer_depth, diffusion):
    field_count, level_count, col_count, row_count = prognostic.shape
    lat_devs = lax.axis_size("lat")
    lon_devs = lax.axis_size("lon")
    lat_total = row_count * lat_devs
    circle_len = col_count * lon_devs
    lat_pos = lax.axis_index("lat")
    lon_pos = lax.axis_index("lon")
    quarter = lat_devs // 4
    is_polar = (lat_pos < quarter) | (lat_pos >= lat_devs - quarter)
    vectors = field_count * level_count
    slab_rows = row_count // lon_devs
    devices = lat_devs * lon_devs
    row_ids = lat_pos * row_count + lon_pos * slab_rows + jnp.arange(slab_rows, dtype=jnp.int32)
    winds_u = lax.dynamic_slice_in_dim(wind_zonal, lon_pos * slab_rows, slab_rows, axis=1)
    winds_v = lax.dynamic_slice_in_dim(wind_merid, lon_pos * slab_rows, slab_rows, axis=1)

    outer, lanes = split_length(circle_len)
    halfway = damping(row_ids, lat_total, circle_len)
    mirrored = halfway[:, 1 : circle_len // 2][:, ::-1]
    full = jnp.concatenate([halfway, mirrored], axis=1)
    by_k = jnp.transpose(full.reshape(slab_rows, lanes, outer), (2, 0, 1))
    by_k = jnp.broadcast_to(by_k[:, None], (outer, vectors, slab_rows, lanes))
    by_k = by_k.reshape(outer, vectors * slab_rows, lanes)
    factors = jnp.concatenate([by_k, by_k], axis=2)

    send = prognostic.reshape(vectors, col_count, lon_devs, slab_rows)
    send = jnp.transpose(send, (2, 1, 0, 3))
    recv = lax.all_to_all(send, "lon", 0, 0, tiled=True)
    state = jnp.transpose(recv, (2, 3, 0, 1)).reshape(
        field_count, level_count, slab_rows, circle_len
    )

    up = [(q, q + 1) for q in range(devices - 1)]
    down = [(q + 1, q) for q in range(devices - 1)]
    row_pos = jnp.arange(slab_rows, dtype=jnp.int32)[None, :, None]
    state = state.reshape(vectors, slab_rows, circle_len)
    for substep in range(ITERS):
        south = lax.ppermute(state[:, -1, :], ("lat", "lon"), up)
        north = lax.ppermute(state[:, 0, :], ("lat", "lon"), down)
        north_rows = jnp.where(
            row_pos == slab_rows - 1, north[:, None, :], jnp.roll(state, -1, axis=1)
        )
        south_rows = jnp.where(row_pos == 0, south[:, None, :], jnp.roll(state, 1, axis=1))
        tendency_now = tendency(
            state,
            north_rows,
            south_rows,
            row_ids,
            lat_total,
            winds_u,
            winds_v,
            layer_depth,
            diffusion,
        )
        flat = tendency_now.reshape(vectors * slab_rows, circle_len)
        filtered = lax.cond(
            is_polar, lambda inner: filter_rows(inner, factors), lambda inner: inner, flat
        )
        state = state + time_step * filtered.reshape(state.shape)

    out = state.reshape(vectors, slab_rows, lon_devs, col_count)
    out = jnp.transpose(out, (2, 3, 0, 1))
    out = lax.all_to_all(out, "lon", 0, 0, tiled=True)
    out = jnp.transpose(out, (2, 1, 0, 3)).reshape(prognostic.shape)
    return out


def solution(mesh):
    return jax.shard_map(
        local,
        mesh=mesh,
        in_specs=(P(None, None, "lon", "lat"), P(None, "lat"), P(None, "lat"), P(), P()),
        out_specs=P(None, None, "lon", "lat"),
        check_vma=False,
    )
```

```python
import math

import jax
import jax.numpy as jnp
from jax import lax
from jax.sharding import PartitionSpec as P

ITERS = 3


time_step = 0.15
precision = lax.Precision.HIGH


def latitude(row_ids, lat_total):
    return (row_ids.astype(jnp.float32) + 0.5) * (math.pi / lat_total) - 0.5 * math.pi


def damping(row_ids, lat_total, circle_len):
    cos_ratio = jnp.cos(latitude(row_ids, lat_total)) / math.cos(0.25 * math.pi)
    wave_ids = jnp.arange(circle_len // 2 + 1)
    sine_vals = jnp.sin(wave_ids.astype(jnp.float32) * (math.pi / circle_len))
    safe_sines = jnp.where(wave_ids == 0, 1.0, sine_vals)
    return jnp.where(
        wave_ids[None, :] == 0, 1.0, jnp.minimum(1.0, cos_ratio[:, None] / safe_sines[None, :])
    )


def tendency(rows, north_rows, south_rows, row_ids, lat_total, winds_u, winds_v, depth, diffusion):
    levels = depth.shape[0]
    fields = rows.shape[0] // levels
    latitudes = latitude(row_ids, lat_total)[:, None]
    cos_centre = jnp.cos(latitudes)
    cos_north = jnp.cos(latitude(row_ids + 1, lat_total))[:, None]
    cos_south = jnp.cos(latitude(row_ids - 1, lat_total))[:, None]
    coriolis = jnp.sin(latitudes)
    wind_u = jnp.tile(winds_u, (fields, 1))[:, :, None]
    wind_v = jnp.tile(winds_v, (fields, 1))[:, :, None]
    east_cols = jnp.roll(rows, -1, axis=2)
    west_cols = jnp.roll(rows, 1, axis=2)
    zonal_diff = (east_cols - west_cols) / (2.0 * cos_centre)
    merid_diff = 0.5 * (north_rows - south_rows)
    advect = wind_u * zonal_diff + wind_v * merid_diff
    u_part = slice(0, levels)
    v_part = slice(levels, 2 * levels)
    h_part = slice(2 * levels, 3 * levels)
    t_part = slice(3 * levels, None)
    diverge = zonal_diff[u_part] + (
        north_rows[v_part] * cos_north - south_rows[v_part] * cos_south
    ) / (2.0 * cos_centre)
    zonal_tend = -advect[u_part] + coriolis * rows[v_part] - zonal_diff[h_part]
    merid_tend = -advect[v_part] - coriolis * rows[u_part] - merid_diff[h_part]
    height_tend = -advect[h_part] - depth[:, None, None] * diverge
    tracer_tend = -advect[t_part] + diffusion.reshape(-1)[:, None, None] * (
        north_rows[t_part] - 2.0 * rows[t_part] + south_rows[t_part]
    )
    return jnp.concatenate([zonal_tend, merid_tend, height_tend, tracer_tend], axis=0)


def trig_pair(rows, cols, length):
    phases = (
        jnp.arange(rows, dtype=jnp.int32)[:, None] * jnp.arange(cols, dtype=jnp.int32)[None, :]
    ) % length
    angles = phases.astype(jnp.float32) * (2.0 * math.pi / length)
    return jnp.cos(angles), jnp.sin(angles)


def mm(spec, left, right):
    return jnp.einsum(spec, left, right, precision=precision)


def split_length(total):
    lanes = 128
    return total // lanes, lanes


def filter_rows(circles, factors):
    count, total = circles.shape
    outer, lanes = split_length(total)
    c_o, s_o = trig_pair(outer, outer, outer)
    c_l, s_l = trig_pair(lanes, lanes, lanes)
    tw_c, tw_s = trig_pair(outer, lanes, total)
    tw_c = tw_c[:, None, :]
    tw_s = tw_s[:, None, :]
    first = jnp.concatenate([c_o, -s_o], axis=0)
    last = jnp.concatenate([c_o, -s_o], axis=1) * (1.0 / total)
    fwd = jnp.concatenate(
        [jnp.concatenate([c_l, -s_l], axis=1), jnp.concatenate([s_l, c_l], axis=1)], axis=0
    )
    inv = jnp.concatenate(
        [jnp.concatenate([c_l, s_l], axis=1), jnp.concatenate([-s_l, c_l], axis=1)], axis=0
    )
    grid = jnp.transpose(circles.reshape(count, outer, lanes), (1, 0, 2))
    spread = mm("ka,af->kf", first, grid.reshape(outer, count * lanes))
    spread = spread.reshape(2, outer, count, lanes)
    b_re = spread[0] * tw_c + spread[1] * tw_s
    b_im = spread[1] * tw_c - spread[0] * tw_s
    joined = jnp.concatenate([b_re, b_im], axis=2)
    spectrum = mm("kcb,bq->kcq", joined, fwd) * factors
    back = mm("kcq,qb->kcb", spectrum, inv)
    d_re = back[:, :, :lanes]
    d_im = back[:, :, lanes:]
    e_re = d_re * tw_c - d_im * tw_s
    e_im = d_im * tw_c + d_re * tw_s
    stacked = jnp.concatenate([e_re, e_im], axis=0).reshape(2 * outer, count * lanes)
    rows = mm("ak,kf->af", last, stacked).reshape(outer, count, lanes)
    return jnp.transpose(rows, (1, 0, 2)).reshape(count, total)


def local(prognostic, wind_zonal, wind_merid, layer_depth, diffusion):
    field_count, level_count, col_count, row_count = prognostic.shape
    lat_devs = lax.axis_size("lat")
    lon_devs = lax.axis_size("lon")
    lat_total = row_count * lat_devs
    circle_len = col_count * lon_devs
    lat_pos = lax.axis_index("lat")
    lon_pos = lax.axis_index("lon")
    quarter = lat_devs // 4
    is_polar = (lat_pos < quarter) | (lat_pos >= lat_devs - quarter)
    vectors = field_count * level_count
    slab_rows = row_count // lon_devs
    devices = lat_devs * lon_devs
    row_ids = lat_pos * row_count + lon_pos * slab_rows + jnp.arange(slab_rows, dtype=jnp.int32)
    winds_u = lax.dynamic_slice_in_dim(wind_zonal, lon_pos * slab_rows, slab_rows, axis=1)
    winds_v = lax.dynamic_slice_in_dim(wind_merid, lon_pos * slab_rows, slab_rows, axis=1)

    outer, lanes = split_length(circle_len)
    halfway = damping(row_ids, lat_total, circle_len)
    mirrored = halfway[:, 1 : circle_len // 2][:, ::-1]
    full = jnp.concatenate([halfway, mirrored], axis=1)
    by_k = jnp.transpose(full.reshape(slab_rows, lanes, outer), (2, 0, 1))
    by_k = jnp.broadcast_to(by_k[:, None], (outer, vectors, slab_rows, lanes))
    by_k = by_k.reshape(outer, vectors * slab_rows, lanes)
    factors = jnp.concatenate([by_k, by_k], axis=2)

    send = prognostic.reshape(vectors, col_count, lon_devs, slab_rows)
    send = jnp.transpose(send, (2, 1, 0, 3))
    recv = lax.all_to_all(send, "lon", 0, 0, tiled=True)
    state = jnp.transpose(recv, (2, 3, 0, 1)).reshape(
        field_count, level_count, slab_rows, circle_len
    )

    up = [(q, q + 1) for q in range(devices - 1)]
    down = [(q + 1, q) for q in range(devices - 1)]
    row_pos = jnp.arange(slab_rows, dtype=jnp.int32)[None, :, None]
    state = lax.optimization_barrier(state.reshape(vectors, slab_rows, circle_len))
    for substep in range(ITERS):
        south = lax.ppermute(state[:, -1, :], ("lat", "lon"), up)
        north = lax.ppermute(state[:, 0, :], ("lat", "lon"), down)
        north_rows = jnp.where(
            row_pos == slab_rows - 1, north[:, None, :], jnp.roll(state, -1, axis=1)
        )
        south_rows = jnp.where(row_pos == 0, south[:, None, :], jnp.roll(state, 1, axis=1))
        tendency_now = tendency(
            state,
            north_rows,
            south_rows,
            row_ids,
            lat_total,
            winds_u,
            winds_v,
            layer_depth,
            diffusion,
        )
        flat = tendency_now.reshape(vectors * slab_rows, circle_len)
        filtered = lax.cond(
            is_polar, lambda inner: filter_rows(inner, factors), lambda inner: inner, flat
        )
        state = state + time_step * filtered.reshape(state.shape)

    out = lax.optimization_barrier(state).reshape(vectors, slab_rows, lon_devs, col_count)
    out = jnp.transpose(out, (2, 3, 0, 1))
    out = lax.all_to_all(out, "lon", 0, 0, tiled=True)
    out = jnp.transpose(out, (2, 1, 0, 3)).reshape(prognostic.shape)
    return out


def solution(mesh):
    return jax.shard_map(
        local,
        mesh=mesh,
        in_specs=(P(None, None, "lon", "lat"), P(None, "lat"), P(None, "lat"), P(), P()),
        out_specs=P(None, None, "lon", "lat"),
        check_vma=False,
    )
```

```python
import math

import jax
import jax.numpy as jnp
from jax import lax
from jax.sharding import PartitionSpec as P

ITERS = 3


time_step = 0.15
precision = lax.Precision.HIGH


def latitude(row_ids, lat_total):
    return (row_ids.astype(jnp.float32) + 0.5) * (math.pi / lat_total) - 0.5 * math.pi


def damping(row_ids, lat_total, circle_len):
    cos_ratio = jnp.cos(latitude(row_ids, lat_total)) / math.cos(0.25 * math.pi)
    wave_ids = jnp.arange(circle_len // 2 + 1)
    sine_vals = jnp.sin(wave_ids.astype(jnp.float32) * (math.pi / circle_len))
    safe_sines = jnp.where(wave_ids == 0, 1.0, sine_vals)
    return jnp.where(
        wave_ids[None, :] == 0, 1.0, jnp.minimum(1.0, cos_ratio[:, None] / safe_sines[None, :])
    )


def shift_cols(tiles, step):
    lanes = tiles.shape[3]
    inside = jnp.roll(tiles, -step, axis=3)
    carried = jnp.roll(inside, -step, axis=0)
    lane_ids = jnp.arange(lanes, dtype=jnp.int32)[None, None, None, :]
    edge = lane_ids == (lanes - 1 if step > 0 else 0)
    return jnp.where(edge, carried, inside)


def tendency(tiles, north_rows, south_rows, row_ids, lat_total, winds_u, winds_v, depth, diffusion):
    levels = depth.shape[0]
    fields = tiles.shape[1] // levels
    latitudes = latitude(row_ids, lat_total)[:, None]
    cos_centre = jnp.cos(latitudes)
    cos_north = jnp.cos(latitude(row_ids + 1, lat_total))[:, None]
    cos_south = jnp.cos(latitude(row_ids - 1, lat_total))[:, None]
    coriolis = jnp.sin(latitudes)
    wind_u = jnp.tile(winds_u, (fields, 1))[:, :, None]
    wind_v = jnp.tile(winds_v, (fields, 1))[:, :, None]
    east_cols = shift_cols(tiles, 1)
    west_cols = shift_cols(tiles, -1)
    zonal_diff = (east_cols - west_cols) / (2.0 * cos_centre)
    merid_diff = 0.5 * (north_rows - south_rows)
    advect = wind_u * zonal_diff + wind_v * merid_diff
    u_part = slice(0, levels)
    v_part = slice(levels, 2 * levels)
    h_part = slice(2 * levels, 3 * levels)
    t_part = slice(3 * levels, None)
    diverge = zonal_diff[:, u_part] + (
        north_rows[:, v_part] * cos_north - south_rows[:, v_part] * cos_south
    ) / (2.0 * cos_centre)
    zonal_tend = -advect[:, u_part] + coriolis * tiles[:, v_part] - zonal_diff[:, h_part]
    merid_tend = -advect[:, v_part] - coriolis * tiles[:, u_part] - merid_diff[:, h_part]
    height_tend = -advect[:, h_part] - depth[:, None, None] * diverge
    tracer_tend = -advect[:, t_part] + diffusion.reshape(-1)[:, None, None] * (
        north_rows[:, t_part] - 2.0 * tiles[:, t_part] + south_rows[:, t_part]
    )
    return jnp.concatenate([zonal_tend, merid_tend, height_tend, tracer_tend], axis=1)


def trig_pair(rows, cols, length):
    phases = (
        jnp.arange(rows, dtype=jnp.int32)[:, None] * jnp.arange(cols, dtype=jnp.int32)[None, :]
    ) % length
    angles = phases.astype(jnp.float32) * (2.0 * math.pi / length)
    return jnp.cos(angles), jnp.sin(angles)


def mm(spec, left, right):
    return jnp.einsum(spec, left, right, precision=precision)


def dft_tables(outer, lanes):
    total = outer * lanes
    c_o, s_o = trig_pair(outer, outer, outer)
    c_l, s_l = trig_pair(lanes, lanes, lanes)
    tw_c, tw_s = trig_pair(outer, lanes, total)
    first = jnp.concatenate([c_o, -s_o], axis=0)
    last = jnp.concatenate([c_o, -s_o], axis=1) * (1.0 / total)
    fwd = jnp.concatenate(
        [jnp.concatenate([c_l, -s_l], axis=1), jnp.concatenate([s_l, c_l], axis=1)], axis=0
    )
    inv = jnp.concatenate(
        [jnp.concatenate([c_l, s_l], axis=1), jnp.concatenate([-s_l, c_l], axis=1)], axis=0
    )
    return first, last, fwd, inv, tw_c[:, None, :], tw_s[:, None, :]


def filter_tiles(grid, factors, tables):
    first, last, fwd, inv, tw_c, tw_s = tables
    outer, count, lanes = grid.shape
    spread = mm("ka,af->kf", first, grid.reshape(outer, count * lanes))
    spread = spread.reshape(2, outer, count, lanes)
    b_re = spread[0] * tw_c + spread[1] * tw_s
    b_im = spread[1] * tw_c - spread[0] * tw_s
    joined = jnp.concatenate([b_re, b_im], axis=2)
    spectrum = mm("kcb,bq->kcq", joined, fwd) * factors
    back = mm("kcq,qb->kcb", spectrum, inv)
    d_re = back[:, :, :lanes]
    d_im = back[:, :, lanes:]
    e_re = d_re * tw_c - d_im * tw_s
    e_im = d_im * tw_c + d_re * tw_s
    stacked = jnp.concatenate([e_re, e_im], axis=0).reshape(2 * outer, count * lanes)
    return mm("ak,kf->af", last, stacked).reshape(outer, count, lanes)


def local(prognostic, wind_zonal, wind_merid, layer_depth, diffusion):
    field_count, level_count, col_count, row_count = prognostic.shape
    lat_devs = lax.axis_size("lat")
    lon_devs = lax.axis_size("lon")
    lat_total = row_count * lat_devs
    circle_len = col_count * lon_devs
    lat_pos = lax.axis_index("lat")
    lon_pos = lax.axis_index("lon")
    quarter = lat_devs // 4
    is_polar = (lat_pos < quarter) | (lat_pos >= lat_devs - quarter)
    vectors = field_count * level_count
    slab_rows = row_count // lon_devs
    devices = lat_devs * lon_devs
    lanes = 128
    outer = circle_len // lanes
    row_ids = lat_pos * row_count + lon_pos * slab_rows + jnp.arange(slab_rows, dtype=jnp.int32)
    winds_u = lax.dynamic_slice_in_dim(wind_zonal, lon_pos * slab_rows, slab_rows, axis=1)
    winds_v = lax.dynamic_slice_in_dim(wind_merid, lon_pos * slab_rows, slab_rows, axis=1)

    halfway = damping(row_ids, lat_total, circle_len)
    mirrored = halfway[:, 1 : circle_len // 2][:, ::-1]
    full = jnp.concatenate([halfway, mirrored], axis=1)
    by_k = jnp.transpose(full.reshape(slab_rows, lanes, outer), (2, 0, 1))
    by_k = jnp.broadcast_to(by_k[:, None], (outer, vectors, slab_rows, lanes))
    by_k = by_k.reshape(outer, vectors * slab_rows, lanes)
    factors = jnp.concatenate([by_k, by_k], axis=2)
    tables = dft_tables(outer, lanes)

    send = prognostic.reshape(vectors, col_count, lon_devs, slab_rows)
    send = jnp.transpose(send, (2, 1, 0, 3))
    recv = lax.all_to_all(send, "lon", 0, 0, tiled=True)
    state = jnp.transpose(recv, (2, 3, 0, 1)).reshape(vectors, slab_rows, outer, lanes)
    state = lax.optimization_barrier(jnp.transpose(state, (2, 0, 1, 3)))

    up = [(q, q + 1) for q in range(devices - 1)]
    down = [(q + 1, q) for q in range(devices - 1)]
    row_pos = jnp.arange(slab_rows, dtype=jnp.int32)[None, None, :, None]
    for substep in range(ITERS):
        south = lax.ppermute(state[:, :, -1, :], ("lat", "lon"), up)
        north = lax.ppermute(state[:, :, 0, :], ("lat", "lon"), down)
        north_rows = jnp.where(
            row_pos == slab_rows - 1, north[:, :, None, :], jnp.roll(state, -1, axis=2)
        )
        south_rows = jnp.where(row_pos == 0, south[:, :, None, :], jnp.roll(state, 1, axis=2))
        tendency_now = tendency(
            state,
            north_rows,
            south_rows,
            row_ids,
            lat_total,
            winds_u,
            winds_v,
            layer_depth,
            diffusion,
        )
        grid = tendency_now.reshape(outer, vectors * slab_rows, lanes)
        filtered = lax.cond(
            is_polar,
            lambda inner, fac, tab: filter_tiles(inner, fac, tab),
            lambda inner, fac, tab: inner,
            grid,
            factors,
            tables,
        )
        state = state + time_step * filtered.reshape(state.shape)

    out = jnp.transpose(lax.optimization_barrier(state), (1, 2, 0, 3))
    out = out.reshape(vectors, slab_rows, lon_devs, col_count)
    out = jnp.transpose(out, (2, 3, 0, 1))
    out = lax.all_to_all(out, "lon", 0, 0, tiled=True)
    out = jnp.transpose(out, (2, 1, 0, 3)).reshape(prognostic.shape)
    return out


def solution(mesh):
    return jax.shard_map(
        local,
        mesh=mesh,
        in_specs=(P(None, None, "lon", "lat"), P(None, "lat"), P(None, "lat"), P(), P()),
        out_specs=P(None, None, "lon", "lat"),
        check_vma=False,
    )
```

```python
import math

import jax
import jax.numpy as jnp
from jax import lax
from jax.sharding import PartitionSpec as P

ITERS = 3


time_step = 0.15
precision = lax.Precision.HIGH


def latitude(row_ids, lat_total):
    return (row_ids.astype(jnp.float32) + 0.5) * (math.pi / lat_total) - 0.5 * math.pi


def damping(row_ids, lat_total, circle_len):
    cos_ratio = jnp.cos(latitude(row_ids, lat_total)) / math.cos(0.25 * math.pi)
    wave_ids = jnp.arange(circle_len // 2 + 1)
    sine_vals = jnp.sin(wave_ids.astype(jnp.float32) * (math.pi / circle_len))
    safe_sines = jnp.where(wave_ids == 0, 1.0, sine_vals)
    return jnp.where(
        wave_ids[None, :] == 0, 1.0, jnp.minimum(1.0, cos_ratio[:, None] / safe_sines[None, :])
    )


def shift_cols(tiles, step):
    lanes = tiles.shape[3]
    inside = jnp.roll(tiles, -step, axis=3)
    carried = jnp.roll(inside, -step, axis=0)
    lane_ids = jnp.arange(lanes, dtype=jnp.int32)[None, None, None, :]
    edge = lane_ids == (lanes - 1 if step > 0 else 0)
    return jnp.where(edge, carried, inside)


def tendency(tiles, north_rows, south_rows, row_ids, lat_total, winds_u, winds_v, depth, diffusion):
    levels = depth.shape[0]
    fields = tiles.shape[1] // levels
    latitudes = latitude(row_ids, lat_total)[:, None]
    cos_centre = jnp.cos(latitudes)
    cos_north = jnp.cos(latitude(row_ids + 1, lat_total))[:, None]
    cos_south = jnp.cos(latitude(row_ids - 1, lat_total))[:, None]
    coriolis = jnp.sin(latitudes)
    wind_u = jnp.tile(winds_u, (fields, 1))[:, :, None]
    wind_v = jnp.tile(winds_v, (fields, 1))[:, :, None]
    east_cols = shift_cols(tiles, 1)
    west_cols = shift_cols(tiles, -1)
    zonal_diff = (east_cols - west_cols) / (2.0 * cos_centre)
    merid_diff = 0.5 * (north_rows - south_rows)
    advect = wind_u * zonal_diff + wind_v * merid_diff
    u_part = slice(0, levels)
    v_part = slice(levels, 2 * levels)
    h_part = slice(2 * levels, 3 * levels)
    t_part = slice(3 * levels, None)
    diverge = zonal_diff[:, u_part] + (
        north_rows[:, v_part] * cos_north - south_rows[:, v_part] * cos_south
    ) / (2.0 * cos_centre)
    zonal_tend = -advect[:, u_part] + coriolis * tiles[:, v_part] - zonal_diff[:, h_part]
    merid_tend = -advect[:, v_part] - coriolis * tiles[:, u_part] - merid_diff[:, h_part]
    height_tend = -advect[:, h_part] - depth[:, None, None] * diverge
    tracer_tend = -advect[:, t_part] + diffusion.reshape(-1)[:, None, None] * (
        north_rows[:, t_part] - 2.0 * tiles[:, t_part] + south_rows[:, t_part]
    )
    return jnp.concatenate([zonal_tend, merid_tend, height_tend, tracer_tend], axis=1)


def trig_pair(rows, cols, length):
    phases = (
        jnp.arange(rows, dtype=jnp.int32)[:, None] * jnp.arange(cols, dtype=jnp.int32)[None, :]
    ) % length
    angles = phases.astype(jnp.float32) * (2.0 * math.pi / length)
    return jnp.cos(angles), jnp.sin(angles)


def mm(spec, left, right):
    return jnp.einsum(spec, left, right, precision=precision)


def dft_tables(outer, lanes):
    total = outer * lanes
    c_o, s_o = trig_pair(outer, outer, outer)
    c_l, s_l = trig_pair(lanes, lanes, lanes)
    tw_c, tw_s = trig_pair(outer, lanes, total)
    first = jnp.concatenate([c_o, -s_o], axis=0)
    last = jnp.concatenate([c_o, -s_o], axis=1) * (1.0 / total)
    fwd = jnp.concatenate(
        [jnp.concatenate([c_l, -s_l], axis=1), jnp.concatenate([s_l, c_l], axis=1)], axis=0
    )
    inv = jnp.concatenate(
        [jnp.concatenate([c_l, s_l], axis=1), jnp.concatenate([-s_l, c_l], axis=1)], axis=0
    )
    return first, last, fwd, inv, tw_c[:, None, :], tw_s[:, None, :]


def filter_tiles(grid, factors, tables):
    first, last, fwd, inv, tw_c, tw_s = tables
    outer, count, lanes = grid.shape
    spread = mm("ka,af->kf", first, grid.reshape(outer, count * lanes))
    spread = spread.reshape(2, outer, count, lanes)
    b_re = spread[0] * tw_c + spread[1] * tw_s
    b_im = spread[1] * tw_c - spread[0] * tw_s
    joined = jnp.concatenate([b_re, b_im], axis=2)
    spectrum = mm("kcb,bq->kcq", joined, fwd) * factors
    back = mm("kcq,qb->kcb", spectrum, inv)
    d_re = back[:, :, :lanes]
    d_im = back[:, :, lanes:]
    e_re = d_re * tw_c - d_im * tw_s
    e_im = d_im * tw_c + d_re * tw_s
    stacked = jnp.concatenate([e_re, e_im], axis=0).reshape(2 * outer, count * lanes)
    return mm("ak,kf->af", last, stacked).reshape(outer, count, lanes)


def slab_path(lon_devs):
    if lon_devs != 16:
        order = list(range(lon_devs))
        if lon_devs >= 4:
            order[2], order[3] = order[3], order[2]
        return order
    path = []
    for y_hi in range(2):
        xs = range(4) if y_hi == 0 else range(3, -1, -1)
        for x in xs:
            cores = (0, 1) if (len(path) // 2) % 2 == 0 else (1, 0)
            for core in cores:
                path.append((y_hi * 4 + x) * 2 + core)
    return path


def local(prognostic, wind_zonal, wind_merid, layer_depth, diffusion):
    field_count, level_count, col_count, row_count = prognostic.shape
    lat_devs = lax.axis_size("lat")
    lon_devs = lax.axis_size("lon")
    lat_total = row_count * lat_devs
    circle_len = col_count * lon_devs
    lat_pos = lax.axis_index("lat")
    lon_pos = lax.axis_index("lon")
    quarter = lat_devs // 4
    is_polar = (lat_pos < quarter) | (lat_pos >= lat_devs - quarter)
    vectors = field_count * level_count
    slab_rows = row_count // lon_devs
    devices = lat_devs * lon_devs
    lanes = 128
    outer = circle_len // lanes
    path = slab_path(lon_devs)
    paths = [path, path[::-1]]
    slots = [[p.index(d) for d in range(lon_devs)] for p in paths]
    parity = lat_pos % 2
    pos_of_slab = jnp.take(jnp.array(paths, dtype=jnp.int32), parity, axis=0)
    slab_of_pos = jnp.take(jnp.array(slots, dtype=jnp.int32), parity, axis=0)
    my_slab = jnp.take(slab_of_pos, lon_pos)
    row_ids = lat_pos * row_count + my_slab * slab_rows + jnp.arange(slab_rows, dtype=jnp.int32)
    winds_u = lax.dynamic_slice_in_dim(wind_zonal, my_slab * slab_rows, slab_rows, axis=1)
    winds_v = lax.dynamic_slice_in_dim(wind_merid, my_slab * slab_rows, slab_rows, axis=1)

    halfway = damping(row_ids, lat_total, circle_len)
    mirrored = halfway[:, 1 : circle_len // 2][:, ::-1]
    full = jnp.concatenate([halfway, mirrored], axis=1)
    by_k = jnp.transpose(full.reshape(slab_rows, lanes, outer), (2, 0, 1))
    by_k = jnp.broadcast_to(by_k[:, None], (outer, vectors, slab_rows, lanes))
    by_k = by_k.reshape(outer, vectors * slab_rows, lanes)
    factors = jnp.concatenate([by_k, by_k], axis=2)
    tables = dft_tables(outer, lanes)

    send = prognostic.reshape(vectors, col_count, lon_devs, slab_rows)
    send = jnp.transpose(send, (2, 1, 0, 3))
    send = jnp.take(send, slab_of_pos, axis=0)
    recv = lax.all_to_all(send, "lon", 0, 0, tiled=True)
    state = jnp.transpose(recv, (2, 3, 0, 1)).reshape(vectors, slab_rows, outer, lanes)
    state = lax.optimization_barrier(jnp.transpose(state, (2, 0, 1, 3)))

    up = []
    for lat in range(lat_devs):
        for slab in range(lon_devs):
            here = lat * lon_devs + paths[lat % 2][slab]
            if slab + 1 < lon_devs:
                up.append((here, lat * lon_devs + paths[lat % 2][slab + 1]))
            elif lat + 1 < lat_devs:
                up.append((here, (lat + 1) * lon_devs + paths[(lat + 1) % 2][0]))
    down = [(b, a) for a, b in up]
    row_pos = jnp.arange(slab_rows, dtype=jnp.int32)[None, None, :, None]
    for substep in range(ITERS):
        south = lax.ppermute(state[:, :, -1, :], ("lat", "lon"), up)
        north = lax.ppermute(state[:, :, 0, :], ("lat", "lon"), down)
        north_rows = jnp.where(
            row_pos == slab_rows - 1, north[:, :, None, :], jnp.roll(state, -1, axis=2)
        )
        south_rows = jnp.where(row_pos == 0, south[:, :, None, :], jnp.roll(state, 1, axis=2))
        tendency_now = tendency(
            state,
            north_rows,
            south_rows,
            row_ids,
            lat_total,
            winds_u,
            winds_v,
            layer_depth,
            diffusion,
        )
        grid = tendency_now.reshape(outer, vectors * slab_rows, lanes)
        filtered = lax.cond(
            is_polar,
            lambda inner, fac, tab: filter_tiles(inner, fac, tab),
            lambda inner, fac, tab: inner,
            grid,
            factors,
            tables,
        )
        state = state + time_step * filtered.reshape(state.shape)

    out = jnp.transpose(lax.optimization_barrier(state), (1, 2, 0, 3))
    out = out.reshape(vectors, slab_rows, lon_devs, col_count)
    out = jnp.transpose(out, (2, 3, 0, 1))
    out = lax.all_to_all(out, "lon", 0, 0, tiled=True)
    out = jnp.take(out, pos_of_slab, axis=0)
    out = jnp.transpose(out, (2, 1, 0, 3)).reshape(prognostic.shape)
    return out


def solution(mesh):
    return jax.shard_map(
        local,
        mesh=mesh,
        in_specs=(P(None, None, "lon", "lat"), P(None, "lat"), P(None, "lat"), P(), P()),
        out_specs=P(None, None, "lon", "lat"),
        check_vma=False,
    )
```

```python
import math

import jax
import jax.numpy as jnp
from jax import lax
from jax.sharding import PartitionSpec as P

ITERS = 3


time_step = 0.15
precision = lax.Precision.HIGH


def latitude(row_ids, lat_total):
    return (row_ids.astype(jnp.float32) + 0.5) * (math.pi / lat_total) - 0.5 * math.pi


def damping(row_ids, lat_total, circle_len):
    cos_ratio = jnp.cos(latitude(row_ids, lat_total)) / math.cos(0.25 * math.pi)
    wave_ids = jnp.arange(circle_len // 2 + 1)
    sine_vals = jnp.sin(wave_ids.astype(jnp.float32) * (math.pi / circle_len))
    safe_sines = jnp.where(wave_ids == 0, 1.0, sine_vals)
    return jnp.where(
        wave_ids[None, :] == 0, 1.0, jnp.minimum(1.0, cos_ratio[:, None] / safe_sines[None, :])
    )


def shift_cols(tiles, step):
    lanes = tiles.shape[3]
    inside = jnp.roll(tiles, -step, axis=3)
    carried = jnp.roll(inside, -step, axis=0)
    lane_ids = jnp.arange(lanes, dtype=jnp.int32)[None, None, None, :]
    edge = lane_ids == (lanes - 1 if step > 0 else 0)
    return jnp.where(edge, carried, inside)


def tendency(tiles, north_rows, south_rows, row_ids, lat_total, winds_u, winds_v, depth, diffusion):
    levels = depth.shape[0]
    fields = tiles.shape[1] // levels
    latitudes = latitude(row_ids, lat_total)[:, None]
    cos_centre = jnp.cos(latitudes)
    cos_north = jnp.cos(latitude(row_ids + 1, lat_total))[:, None]
    cos_south = jnp.cos(latitude(row_ids - 1, lat_total))[:, None]
    coriolis = jnp.sin(latitudes)
    wind_u = jnp.tile(winds_u, (fields, 1))[:, :, None]
    wind_v = jnp.tile(winds_v, (fields, 1))[:, :, None]
    east_cols = shift_cols(tiles, 1)
    west_cols = shift_cols(tiles, -1)
    zonal_diff = (east_cols - west_cols) / (2.0 * cos_centre)
    merid_diff = 0.5 * (north_rows - south_rows)
    advect = wind_u * zonal_diff + wind_v * merid_diff
    u_part = slice(0, levels)
    v_part = slice(levels, 2 * levels)
    h_part = slice(2 * levels, 3 * levels)
    t_part = slice(3 * levels, None)
    diverge = zonal_diff[:, u_part] + (
        north_rows[:, v_part] * cos_north - south_rows[:, v_part] * cos_south
    ) / (2.0 * cos_centre)
    zonal_tend = -advect[:, u_part] + coriolis * tiles[:, v_part] - zonal_diff[:, h_part]
    merid_tend = -advect[:, v_part] - coriolis * tiles[:, u_part] - merid_diff[:, h_part]
    height_tend = -advect[:, h_part] - depth[:, None, None] * diverge
    tracer_tend = -advect[:, t_part] + diffusion.reshape(-1)[:, None, None] * (
        north_rows[:, t_part] - 2.0 * tiles[:, t_part] + south_rows[:, t_part]
    )
    return jnp.concatenate([zonal_tend, merid_tend, height_tend, tracer_tend], axis=1)


def trig_pair(rows, cols, length):
    phases = (
        jnp.arange(rows, dtype=jnp.int32)[:, None] * jnp.arange(cols, dtype=jnp.int32)[None, :]
    ) % length
    angles = phases.astype(jnp.float32) * (2.0 * math.pi / length)
    return jnp.cos(angles), jnp.sin(angles)


def mm(spec, left, right):
    return jnp.einsum(spec, left, right, precision=precision)


def dft_tables(outer, lanes):
    total = outer * lanes
    c_o, s_o = trig_pair(outer, outer, outer)
    c_l, s_l = trig_pair(lanes, lanes, lanes)
    tw_c, tw_s = trig_pair(outer, lanes, total)
    first = jnp.concatenate([c_o, -s_o], axis=0)
    last = jnp.concatenate([c_o, -s_o], axis=1) * (1.0 / total)
    fwd = jnp.concatenate(
        [jnp.concatenate([c_l, -s_l], axis=1), jnp.concatenate([s_l, c_l], axis=1)], axis=0
    )
    inv = jnp.concatenate(
        [jnp.concatenate([c_l, s_l], axis=1), jnp.concatenate([-s_l, c_l], axis=1)], axis=0
    )
    return first, last, fwd, inv, tw_c[:, None, :], tw_s[:, None, :]


def filter_tiles(grid, factors, tables):
    first, last, fwd, inv, tw_c, tw_s = tables
    outer, count, lanes = grid.shape
    half = count // 2
    spread = mm("ka,af->kf", first, grid.reshape(outer, count * lanes))
    spread = spread.reshape(2, outer, count, lanes)
    a_re = spread[0][:, :half] - spread[1][:, half:]
    a_im = spread[0][:, half:] + spread[1][:, :half]
    b_re = a_re * tw_c + a_im * tw_s
    b_im = a_im * tw_c - a_re * tw_s
    joined = jnp.concatenate([b_re, b_im], axis=2)
    spectrum = mm("kcb,bq->kcq", joined, fwd) * factors[:, :half]
    back = mm("kcq,qb->kcb", spectrum, inv)
    d_re = back[:, :, :lanes]
    d_im = back[:, :, lanes:]
    e_re = d_re * tw_c - d_im * tw_s
    e_im = d_im * tw_c + d_re * tw_s
    stacked = jnp.stack(
        [jnp.concatenate([e_re, e_im], axis=1), jnp.concatenate([e_im, -e_re], axis=1)], axis=0
    ).reshape(2 * outer, count * lanes)
    return mm("ak,kf->af", last, stacked).reshape(outer, count, lanes)


def slab_path(lon_devs):
    if lon_devs != 16:
        order = list(range(lon_devs))
        if lon_devs >= 4:
            order[2], order[3] = order[3], order[2]
        return order
    path = []
    for y_hi in range(2):
        xs = range(4) if y_hi == 0 else range(3, -1, -1)
        for x in xs:
            cores = (0, 1) if (len(path) // 2) % 2 == 0 else (1, 0)
            for core in cores:
                path.append((y_hi * 4 + x) * 2 + core)
    return path


def local(prognostic, wind_zonal, wind_merid, layer_depth, diffusion):
    field_count, level_count, col_count, row_count = prognostic.shape
    lat_devs = lax.axis_size("lat")
    lon_devs = lax.axis_size("lon")
    lat_total = row_count * lat_devs
    circle_len = col_count * lon_devs
    lat_pos = lax.axis_index("lat")
    lon_pos = lax.axis_index("lon")
    quarter = lat_devs // 4
    is_polar = (lat_pos < quarter) | (lat_pos >= lat_devs - quarter)
    vectors = field_count * level_count
    slab_rows = row_count // lon_devs
    devices = lat_devs * lon_devs
    lanes = 128
    outer = circle_len // lanes
    path = slab_path(lon_devs)
    paths = [path, path[::-1]]
    slots = [[p.index(d) for d in range(lon_devs)] for p in paths]
    parity = lat_pos % 2
    pos_of_slab = jnp.take(jnp.array(paths, dtype=jnp.int32), parity, axis=0)
    slab_of_pos = jnp.take(jnp.array(slots, dtype=jnp.int32), parity, axis=0)
    my_slab = jnp.take(slab_of_pos, lon_pos)
    row_ids = lat_pos * row_count + my_slab * slab_rows + jnp.arange(slab_rows, dtype=jnp.int32)
    winds_u = lax.dynamic_slice_in_dim(wind_zonal, my_slab * slab_rows, slab_rows, axis=1)
    winds_v = lax.dynamic_slice_in_dim(wind_merid, my_slab * slab_rows, slab_rows, axis=1)

    halfway = damping(row_ids, lat_total, circle_len)
    mirrored = halfway[:, 1 : circle_len // 2][:, ::-1]
    full = jnp.concatenate([halfway, mirrored], axis=1)
    by_k = jnp.transpose(full.reshape(slab_rows, lanes, outer), (2, 0, 1))
    by_k = jnp.broadcast_to(by_k[:, None], (outer, vectors, slab_rows, lanes))
    by_k = by_k.reshape(outer, vectors * slab_rows, lanes)
    factors = jnp.concatenate([by_k, by_k], axis=2)
    tables = dft_tables(outer, lanes)

    send = prognostic.reshape(vectors, col_count, lon_devs, slab_rows)
    send = jnp.transpose(send, (2, 1, 0, 3))
    send = jnp.take(send, slab_of_pos, axis=0)
    recv = lax.all_to_all(send, "lon", 0, 0, tiled=True)
    state = jnp.transpose(recv, (2, 3, 0, 1)).reshape(vectors, slab_rows, outer, lanes)
    state = lax.optimization_barrier(jnp.transpose(state, (2, 0, 1, 3)))

    up = []
    for lat in range(lat_devs):
        for slab in range(lon_devs):
            here = lat * lon_devs + paths[lat % 2][slab]
            if slab + 1 < lon_devs:
                up.append((here, lat * lon_devs + paths[lat % 2][slab + 1]))
            elif lat + 1 < lat_devs:
                up.append((here, (lat + 1) * lon_devs + paths[(lat + 1) % 2][0]))
    down = [(b, a) for a, b in up]
    row_pos = jnp.arange(slab_rows, dtype=jnp.int32)[None, None, :, None]
    for substep in range(ITERS):
        south = lax.ppermute(state[:, :, -1, :], ("lat", "lon"), up)
        north = lax.ppermute(state[:, :, 0, :], ("lat", "lon"), down)
        north_rows = jnp.where(
            row_pos == slab_rows - 1, north[:, :, None, :], jnp.roll(state, -1, axis=2)
        )
        south_rows = jnp.where(row_pos == 0, south[:, :, None, :], jnp.roll(state, 1, axis=2))
        tendency_now = tendency(
            state,
            north_rows,
            south_rows,
            row_ids,
            lat_total,
            winds_u,
            winds_v,
            layer_depth,
            diffusion,
        )
        grid = tendency_now.reshape(outer, vectors * slab_rows, lanes)
        filtered = lax.cond(
            is_polar,
            lambda inner, fac, tab: filter_tiles(inner, fac, tab),
            lambda inner, fac, tab: inner,
            grid,
            factors,
            tables,
        )
        state = state + time_step * filtered.reshape(state.shape)

    out = jnp.transpose(lax.optimization_barrier(state), (1, 2, 0, 3))
    out = out.reshape(vectors, slab_rows, lon_devs, col_count)
    out = jnp.transpose(out, (2, 3, 0, 1))
    out = lax.all_to_all(out, "lon", 0, 0, tiled=True)
    out = jnp.take(out, pos_of_slab, axis=0)
    out = jnp.transpose(out, (2, 1, 0, 3)).reshape(prognostic.shape)
    return out


def solution(mesh):
    return jax.shard_map(
        local,
        mesh=mesh,
        in_specs=(P(None, None, "lon", "lat"), P(None, "lat"), P(None, "lat"), P(), P()),
        out_specs=P(None, None, "lon", "lat"),
        check_vma=False,
    )
```

```python
import math

import jax
import jax.numpy as jnp
from jax import lax
from jax.sharding import PartitionSpec as P

ITERS = 3


time_step = 0.15
precision = lax.Precision.HIGH


def latitude(row_ids, lat_total):
    return (row_ids.astype(jnp.float32) + 0.5) * (math.pi / lat_total) - 0.5 * math.pi


def damping(row_ids, lat_total, circle_len):
    cos_ratio = jnp.cos(latitude(row_ids, lat_total)) / math.cos(0.25 * math.pi)
    wave_ids = jnp.arange(circle_len // 2 + 1)
    sine_vals = jnp.sin(wave_ids.astype(jnp.float32) * (math.pi / circle_len))
    safe_sines = jnp.where(wave_ids == 0, 1.0, sine_vals)
    return jnp.where(
        wave_ids[None, :] == 0, 1.0, jnp.minimum(1.0, cos_ratio[:, None] / safe_sines[None, :])
    )


def shift_cols(tiles, step):
    lanes = tiles.shape[3]
    inside = jnp.roll(tiles, -step, axis=3)
    carried = jnp.roll(inside, -step, axis=0)
    lane_ids = jnp.arange(lanes, dtype=jnp.int32)[None, None, None, :]
    edge = lane_ids == (lanes - 1 if step > 0 else 0)
    return jnp.where(edge, carried, inside)


def tendency(tiles, north_rows, south_rows, row_ids, lat_total, winds_u, winds_v, depth, diffusion):
    levels = depth.shape[0]
    fields = tiles.shape[1] // levels
    latitudes = latitude(row_ids, lat_total)[:, None]
    cos_centre = jnp.cos(latitudes)
    cos_north = jnp.cos(latitude(row_ids + 1, lat_total))[:, None]
    cos_south = jnp.cos(latitude(row_ids - 1, lat_total))[:, None]
    coriolis = jnp.sin(latitudes)
    wind_u = jnp.tile(winds_u, (fields, 1))[:, :, None]
    wind_v = jnp.tile(winds_v, (fields, 1))[:, :, None]
    east_cols = shift_cols(tiles, 1)
    west_cols = shift_cols(tiles, -1)
    zonal_diff = (east_cols - west_cols) / (2.0 * cos_centre)
    merid_diff = 0.5 * (north_rows - south_rows)
    advect = wind_u * zonal_diff + wind_v * merid_diff
    u_part = slice(0, levels)
    v_part = slice(levels, 2 * levels)
    h_part = slice(2 * levels, 3 * levels)
    t_part = slice(3 * levels, None)
    diverge = zonal_diff[:, u_part] + (
        north_rows[:, v_part] * cos_north - south_rows[:, v_part] * cos_south
    ) / (2.0 * cos_centre)
    zonal_tend = -advect[:, u_part] + coriolis * tiles[:, v_part] - zonal_diff[:, h_part]
    merid_tend = -advect[:, v_part] - coriolis * tiles[:, u_part] - merid_diff[:, h_part]
    height_tend = -advect[:, h_part] - depth[:, None, None] * diverge
    tracer_tend = -advect[:, t_part] + diffusion.reshape(-1)[:, None, None] * (
        north_rows[:, t_part] - 2.0 * tiles[:, t_part] + south_rows[:, t_part]
    )
    return jnp.concatenate([zonal_tend, merid_tend, height_tend, tracer_tend], axis=1)


def trig_pair(rows, cols, length):
    phases = (
        jnp.arange(rows, dtype=jnp.int32)[:, None] * jnp.arange(cols, dtype=jnp.int32)[None, :]
    ) % length
    angles = phases.astype(jnp.float32) * (2.0 * math.pi / length)
    return jnp.cos(angles), jnp.sin(angles)


def mm(spec, left, right):
    return jnp.einsum(spec, left, right, precision=precision)


def dft_tables(outer, lanes):
    total = outer * lanes
    c_o, s_o = trig_pair(outer, outer, outer)
    c_l, s_l = trig_pair(lanes, lanes, lanes)
    tw_c, tw_s = trig_pair(outer, lanes, total)
    first = jnp.concatenate([c_o, -s_o], axis=0)
    last = jnp.concatenate([c_o, -s_o], axis=1) * (1.0 / total)
    fwd = jnp.concatenate(
        [jnp.concatenate([c_l, -s_l], axis=1), jnp.concatenate([s_l, c_l], axis=1)], axis=0
    )
    inv = jnp.concatenate(
        [jnp.concatenate([c_l, s_l], axis=1), jnp.concatenate([-s_l, c_l], axis=1)], axis=0
    )
    return first, last, fwd, inv, tw_c[:, None, :], tw_s[:, None, :]


def filter_tiles(grid, factors, tables):
    first, last, fwd, inv, tw_c, tw_s = tables
    outer, count, lanes = grid.shape
    half = count // 2
    spread = mm("ka,af->kf", first, grid.reshape(outer, count * lanes))
    spread = spread.reshape(2, outer, count, lanes)
    a_re = spread[0][:, :half] - spread[1][:, half:]
    a_im = spread[0][:, half:] + spread[1][:, :half]
    b_re = a_re * tw_c + a_im * tw_s
    b_im = a_im * tw_c - a_re * tw_s
    joined = jnp.concatenate([b_re, b_im], axis=2)
    spectrum = mm("kcb,bq->kcq", joined, fwd) * factors[:, :half]
    back = mm("kcq,qb->kcb", spectrum, inv)
    d_re = back[:, :, :lanes]
    d_im = back[:, :, lanes:]
    e_re = d_re * tw_c - d_im * tw_s
    e_im = d_im * tw_c + d_re * tw_s
    stacked = jnp.stack(
        [jnp.concatenate([e_re, e_im], axis=1), jnp.concatenate([e_im, -e_re], axis=1)], axis=0
    ).reshape(2 * outer, count * lanes)
    return mm("ak,kf->af", last, stacked).reshape(outer, count, lanes)


def slab_path(lon_devs):
    if lon_devs != 16:
        order = list(range(lon_devs))
        if lon_devs >= 4:
            order[2], order[3] = order[3], order[2]
        return order
    path = []
    for y_hi in range(2):
        xs = range(4) if y_hi == 0 else range(3, -1, -1)
        for x in xs:
            cores = (0, 1) if (len(path) // 2) % 2 == 0 else (1, 0)
            for core in cores:
                path.append((y_hi * 4 + x) * 2 + core)
    return path


def local(prognostic, wind_zonal, wind_merid, layer_depth, diffusion):
    field_count, level_count, col_count, row_count = prognostic.shape
    lat_devs = lax.axis_size("lat")
    lon_devs = lax.axis_size("lon")
    lat_total = row_count * lat_devs
    circle_len = col_count * lon_devs
    lat_pos = lax.axis_index("lat")
    lon_pos = lax.axis_index("lon")
    quarter = lat_devs // 4
    is_polar = (lat_pos < quarter) | (lat_pos >= lat_devs - quarter)
    vectors = field_count * level_count
    slab_rows = row_count // lon_devs
    devices = lat_devs * lon_devs
    lanes = 128
    outer = circle_len // lanes
    path = slab_path(lon_devs)
    paths = [path, path[::-1]]
    slots = [[p.index(d) for d in range(lon_devs)] for p in paths]
    parity = lat_pos % 2
    pos_of_slab = jnp.take(jnp.array(paths, dtype=jnp.int32), parity, axis=0)
    slab_of_pos = jnp.take(jnp.array(slots, dtype=jnp.int32), parity, axis=0)
    my_slab = jnp.take(slab_of_pos, lon_pos)
    row_ids = lat_pos * row_count + my_slab * slab_rows + jnp.arange(slab_rows, dtype=jnp.int32)
    winds_u = lax.dynamic_slice_in_dim(wind_zonal, my_slab * slab_rows, slab_rows, axis=1)
    winds_v = lax.dynamic_slice_in_dim(wind_merid, my_slab * slab_rows, slab_rows, axis=1)

    halfway = damping(row_ids, lat_total, circle_len)
    mirrored = halfway[:, 1 : circle_len // 2][:, ::-1]
    full = jnp.concatenate([halfway, mirrored], axis=1)
    by_k = jnp.transpose(full.reshape(slab_rows, lanes, outer), (2, 0, 1))
    by_k = jnp.broadcast_to(by_k[:, None], (outer, vectors, slab_rows, lanes))
    by_k = by_k.reshape(outer, vectors * slab_rows, lanes)
    factors = jnp.concatenate([by_k, by_k], axis=2)
    tables = dft_tables(outer, lanes)

    send = prognostic.reshape(vectors, col_count, lon_devs, slab_rows)
    send = jnp.transpose(send, (2, 1, 0, 3))
    send = jnp.take(send, slab_of_pos, axis=0)
    recv = lax.all_to_all(send, "lon", 0, 0, tiled=True)
    state = jnp.transpose(recv, (2, 3, 0, 1)).reshape(vectors, slab_rows, outer, lanes)
    state = lax.optimization_barrier(jnp.transpose(state, (2, 0, 1, 3)))

    up = []
    for lat in range(lat_devs):
        for slab in range(lon_devs):
            here = lat * lon_devs + paths[lat % 2][slab]
            if slab + 1 < lon_devs:
                up.append((here, lat * lon_devs + paths[lat % 2][slab + 1]))
            elif lat + 1 < lat_devs:
                up.append((here, (lat + 1) * lon_devs + paths[(lat + 1) % 2][0]))
    down = [(b, a) for a, b in up]
    row_pos = jnp.arange(slab_rows, dtype=jnp.int32)[None, None, :, None]
    def substep(step, state):
        south = lax.ppermute(state[:, :, -1, :], ("lat", "lon"), up)
        north = lax.ppermute(state[:, :, 0, :], ("lat", "lon"), down)
        north_rows = jnp.where(
            row_pos == slab_rows - 1, north[:, :, None, :], jnp.roll(state, -1, axis=2)
        )
        south_rows = jnp.where(row_pos == 0, south[:, :, None, :], jnp.roll(state, 1, axis=2))
        tendency_now = tendency(
            state,
            north_rows,
            south_rows,
            row_ids,
            lat_total,
            winds_u,
            winds_v,
            layer_depth,
            diffusion,
        )
        grid = tendency_now.reshape(outer, vectors * slab_rows, lanes)
        filtered = lax.cond(
            is_polar,
            lambda inner, fac, tab: filter_tiles(inner, fac, tab),
            lambda inner, fac, tab: inner,
            grid,
            factors,
            tables,
        )
        state = state + time_step * filtered.reshape(state.shape)
        return state

    state = lax.fori_loop(0, ITERS, substep, state)

    out = jnp.transpose(lax.optimization_barrier(state), (1, 2, 0, 3))
    out = out.reshape(vectors, slab_rows, lon_devs, col_count)
    out = jnp.transpose(out, (2, 3, 0, 1))
    out = lax.all_to_all(out, "lon", 0, 0, tiled=True)
    out = jnp.take(out, pos_of_slab, axis=0)
    out = jnp.transpose(out, (2, 1, 0, 3)).reshape(prognostic.shape)
    return out


def solution(mesh):
    return jax.shard_map(
        local,
        mesh=mesh,
        in_specs=(P(None, None, "lon", "lat"), P(None, "lat"), P(None, "lat"), P(), P()),
        out_specs=P(None, None, "lon", "lat"),
        check_vma=False,
    )
```

```python
import math

import jax
import jax.numpy as jnp
from jax import lax
from jax.sharding import PartitionSpec as P

ITERS = 3


time_step = 0.15
precision = lax.Precision.HIGH


def latitude(row_ids, lat_total):
    return (row_ids.astype(jnp.float32) + 0.5) * (math.pi / lat_total) - 0.5 * math.pi


def damping(row_ids, lat_total, circle_len):
    cos_ratio = jnp.cos(latitude(row_ids, lat_total)) / math.cos(0.25 * math.pi)
    wave_ids = jnp.arange(circle_len // 2 + 1)
    sine_vals = jnp.sin(wave_ids.astype(jnp.float32) * (math.pi / circle_len))
    safe_sines = jnp.where(wave_ids == 0, 1.0, sine_vals)
    return jnp.where(
        wave_ids[None, :] == 0, 1.0, jnp.minimum(1.0, cos_ratio[:, None] / safe_sines[None, :])
    )


def shift_cols(tiles, step):
    lanes = tiles.shape[3]
    inside = jnp.roll(tiles, -step, axis=3)
    carried = jnp.roll(inside, -step, axis=0)
    lane_ids = jnp.arange(lanes, dtype=jnp.int32)[None, None, None, :]
    edge = lane_ids == (lanes - 1 if step > 0 else 0)
    return jnp.where(edge, carried, inside)


def tendency(tiles, north_rows, south_rows, row_ids, lat_total, winds_u, winds_v, depth, diffusion):
    levels = depth.shape[0]
    fields = tiles.shape[1] // levels
    latitudes = latitude(row_ids, lat_total)[:, None]
    cos_centre = jnp.cos(latitudes)
    cos_north = jnp.cos(latitude(row_ids + 1, lat_total))[:, None]
    cos_south = jnp.cos(latitude(row_ids - 1, lat_total))[:, None]
    coriolis = jnp.sin(latitudes)
    wind_u = jnp.tile(winds_u, (fields, 1))[:, :, None]
    wind_v = jnp.tile(winds_v, (fields, 1))[:, :, None]
    east_cols = shift_cols(tiles, 1)
    west_cols = shift_cols(tiles, -1)
    zonal_diff = (east_cols - west_cols) / (2.0 * cos_centre)
    merid_diff = 0.5 * (north_rows - south_rows)
    advect = wind_u * zonal_diff + wind_v * merid_diff
    u_part = slice(0, levels)
    v_part = slice(levels, 2 * levels)
    h_part = slice(2 * levels, 3 * levels)
    t_part = slice(3 * levels, None)
    diverge = zonal_diff[:, u_part] + (
        north_rows[:, v_part] * cos_north - south_rows[:, v_part] * cos_south
    ) / (2.0 * cos_centre)
    zonal_tend = -advect[:, u_part] + coriolis * tiles[:, v_part] - zonal_diff[:, h_part]
    merid_tend = -advect[:, v_part] - coriolis * tiles[:, u_part] - merid_diff[:, h_part]
    height_tend = -advect[:, h_part] - depth[:, None, None] * diverge
    tracer_tend = -advect[:, t_part] + diffusion.reshape(-1)[:, None, None] * (
        north_rows[:, t_part] - 2.0 * tiles[:, t_part] + south_rows[:, t_part]
    )
    return jnp.concatenate([zonal_tend, merid_tend, height_tend, tracer_tend], axis=1)


def trig_pair(rows, cols, length):
    phases = (
        jnp.arange(rows, dtype=jnp.int32)[:, None] * jnp.arange(cols, dtype=jnp.int32)[None, :]
    ) % length
    angles = phases.astype(jnp.float32) * (2.0 * math.pi / length)
    return jnp.cos(angles), jnp.sin(angles)


def mm(spec, left, right):
    return jnp.einsum(spec, left, right, precision=precision)


def dft_tables(outer, lanes):
    total = outer * lanes
    c_o, s_o = trig_pair(outer, outer, outer)
    c_l, s_l = trig_pair(lanes, lanes, lanes)
    tw_c, tw_s = trig_pair(outer, lanes, total)
    first = jnp.concatenate([c_o, -s_o], axis=0)
    last = jnp.concatenate([c_o, -s_o], axis=1) * (1.0 / total)
    fwd = jnp.concatenate(
        [jnp.concatenate([c_l, -s_l], axis=1), jnp.concatenate([s_l, c_l], axis=1)], axis=0
    )
    inv = jnp.concatenate(
        [jnp.concatenate([c_l, s_l], axis=1), jnp.concatenate([-s_l, c_l], axis=1)], axis=0
    )
    return first, last, fwd, inv, tw_c[:, None, :], tw_s[:, None, :]


def filter_tiles(grid, factors, tables):
    first, last, fwd, inv, tw_c, tw_s = tables
    outer, count, lanes = grid.shape
    half = count // 2
    spread = mm("ka,af->kf", first, grid.reshape(outer, count * lanes))
    spread = spread.reshape(2, outer, count, lanes)
    a_re = spread[0][:, :half] - spread[1][:, half:]
    a_im = spread[0][:, half:] + spread[1][:, :half]
    b_re = a_re * tw_c + a_im * tw_s
    b_im = a_im * tw_c - a_re * tw_s
    joined = jnp.concatenate([b_re, b_im], axis=2)
    spectrum = mm("kcb,bq->kcq", joined, fwd) * factors[:, :half]
    back = mm("kcq,qb->kcb", spectrum, inv)
    d_re = back[:, :, :lanes]
    d_im = back[:, :, lanes:]
    e_re = d_re * tw_c - d_im * tw_s
    e_im = d_im * tw_c + d_re * tw_s
    stacked = jnp.stack(
        [jnp.concatenate([e_re, e_im], axis=1), jnp.concatenate([e_im, -e_re], axis=1)], axis=0
    ).reshape(2 * outer, count * lanes)
    return mm("ak,kf->af", last, stacked).reshape(outer, count, lanes)


def slab_path(lon_devs):
    if lon_devs != 16:
        order = list(range(lon_devs))
        if lon_devs >= 4:
            order[2], order[3] = order[3], order[2]
        return order
    path = []
    for y_hi in range(2):
        xs = range(4) if y_hi == 0 else range(3, -1, -1)
        for x in xs:
            cores = (0, 1) if (len(path) // 2) % 2 == 0 else (1, 0)
            for core in cores:
                path.append((y_hi * 4 + x) * 2 + core)
    return path


def local(prognostic, wind_zonal, wind_merid, layer_depth, diffusion):
    field_count, level_count, col_count, row_count = prognostic.shape
    lat_devs = lax.axis_size("lat")
    lon_devs = lax.axis_size("lon")
    lat_total = row_count * lat_devs
    circle_len = col_count * lon_devs
    lat_pos = lax.axis_index("lat")
    lon_pos = lax.axis_index("lon")
    quarter = lat_devs // 4
    is_polar = (lat_pos < quarter) | (lat_pos >= lat_devs - quarter)
    vectors = field_count * level_count
    slab_rows = row_count // lon_devs
    devices = lat_devs * lon_devs
    lanes = 128
    outer = circle_len // lanes
    path = slab_path(lon_devs)
    paths = [path, path[::-1]]
    slots = [[p.index(d) for d in range(lon_devs)] for p in paths]
    parity = lat_pos % 2
    pos_of_slab = jnp.take(jnp.array(paths, dtype=jnp.int32), parity, axis=0)
    slab_of_pos = jnp.take(jnp.array(slots, dtype=jnp.int32), parity, axis=0)
    my_slab = jnp.take(slab_of_pos, lon_pos)
    row_ids = lat_pos * row_count + my_slab * slab_rows + jnp.arange(slab_rows, dtype=jnp.int32)
    winds_u = lax.dynamic_slice_in_dim(wind_zonal, my_slab * slab_rows, slab_rows, axis=1)
    winds_v = lax.dynamic_slice_in_dim(wind_merid, my_slab * slab_rows, slab_rows, axis=1)

    halfway = damping(row_ids, lat_total, circle_len)
    mirrored = halfway[:, 1 : circle_len // 2][:, ::-1]
    full = jnp.concatenate([halfway, mirrored], axis=1)
    by_k = jnp.transpose(full.reshape(slab_rows, lanes, outer), (2, 0, 1))
    by_k = jnp.broadcast_to(by_k[:, None], (outer, vectors, slab_rows, lanes))
    by_k = by_k.reshape(outer, vectors * slab_rows, lanes)
    factors = jnp.concatenate([by_k, by_k], axis=2)
    tables = dft_tables(outer, lanes)

    send = prognostic.reshape(vectors, col_count, lon_devs, slab_rows)
    send = jnp.transpose(send, (2, 1, 0, 3))
    send = jnp.take(send, slab_of_pos, axis=0)
    recv = lax.all_to_all(send, "lon", 0, 0, tiled=True)
    state = jnp.transpose(recv, (2, 3, 0, 1)).reshape(vectors, slab_rows, outer, lanes)
    state = lax.optimization_barrier(jnp.transpose(state, (2, 0, 1, 3)))

    up = []
    for lat in range(lat_devs):
        for slab in range(lon_devs):
            here = lat * lon_devs + paths[lat % 2][slab]
            if slab + 1 < lon_devs:
                up.append((here, lat * lon_devs + paths[lat % 2][slab + 1]))
            elif lat + 1 < lat_devs:
                up.append((here, (lat + 1) * lon_devs + paths[(lat + 1) % 2][0]))
    down = [(b, a) for a, b in up]
    row_pos = jnp.arange(slab_rows, dtype=jnp.int32)[None, None, :, None]
    for substep in range(ITERS):
        edge_shape = (outer, vectors, lanes)
        dense = (outer * vectors, lanes)
        south = lax.ppermute(state[:, :, -1, :].reshape(dense), ("lat", "lon"), up)
        north = lax.ppermute(state[:, :, 0, :].reshape(dense), ("lat", "lon"), down)
        south = south.reshape(edge_shape)
        north = north.reshape(edge_shape)
        north_rows = jnp.where(
            row_pos == slab_rows - 1, north[:, :, None, :], jnp.roll(state, -1, axis=2)
        )
        south_rows = jnp.where(row_pos == 0, south[:, :, None, :], jnp.roll(state, 1, axis=2))
        tendency_now = tendency(
            state,
            north_rows,
            south_rows,
            row_ids,
            lat_total,
            winds_u,
            winds_v,
            layer_depth,
            diffusion,
        )
        grid = tendency_now.reshape(outer, vectors * slab_rows, lanes)
        filtered = lax.cond(
            is_polar,
            lambda inner, fac, tab: filter_tiles(inner, fac, tab),
            lambda inner, fac, tab: inner,
            grid,
            factors,
            tables,
        )
        state = state + time_step * filtered.reshape(state.shape)

    out = jnp.transpose(lax.optimization_barrier(state), (1, 2, 0, 3))
    out = out.reshape(vectors, slab_rows, lon_devs, col_count)
    out = jnp.transpose(out, (2, 3, 0, 1))
    out = lax.all_to_all(out, "lon", 0, 0, tiled=True)
    out = jnp.take(out, pos_of_slab, axis=0)
    out = jnp.transpose(out, (2, 1, 0, 3)).reshape(prognostic.shape)
    return out


def solution(mesh):
    return jax.shard_map(
        local,
        mesh=mesh,
        in_specs=(P(None, None, "lon", "lat"), P(None, "lat"), P(None, "lat"), P(), P()),
        out_specs=P(None, None, "lon", "lat"),
        check_vma=False,
    )
```

```python
import math

import jax
import jax.numpy as jnp
from jax import lax
from jax.sharding import PartitionSpec as P

ITERS = 3


time_step = 0.15
precision = lax.Precision.HIGH


def latitude(row_ids, lat_total):
    return (row_ids.astype(jnp.float32) + 0.5) * (math.pi / lat_total) - 0.5 * math.pi


def damping(row_ids, lat_total, circle_len):
    cos_ratio = jnp.cos(latitude(row_ids, lat_total)) / math.cos(0.25 * math.pi)
    wave_ids = jnp.arange(circle_len // 2 + 1)
    sine_vals = jnp.sin(wave_ids.astype(jnp.float32) * (math.pi / circle_len))
    safe_sines = jnp.where(wave_ids == 0, 1.0, sine_vals)
    return jnp.where(
        wave_ids[None, :] == 0, 1.0, jnp.minimum(1.0, cos_ratio[:, None] / safe_sines[None, :])
    )


def shift_cols(tiles, step):
    lanes = tiles.shape[3]
    inside = jnp.roll(tiles, -step, axis=3)
    carried = jnp.roll(inside, -step, axis=0)
    lane_ids = jnp.arange(lanes, dtype=jnp.int32)[None, None, None, :]
    edge = lane_ids == (lanes - 1 if step > 0 else 0)
    return jnp.where(edge, carried, inside)


def tendency(tiles, north_rows, south_rows, row_ids, lat_total, winds_u, winds_v, depth, diffusion):
    levels = depth.shape[0]
    fields = tiles.shape[1] // levels
    latitudes = latitude(row_ids, lat_total)[:, None]
    cos_centre = jnp.cos(latitudes)
    cos_north = jnp.cos(latitude(row_ids + 1, lat_total))[:, None]
    cos_south = jnp.cos(latitude(row_ids - 1, lat_total))[:, None]
    coriolis = jnp.sin(latitudes)
    wind_u = jnp.tile(winds_u, (fields, 1))[:, :, None]
    wind_v = jnp.tile(winds_v, (fields, 1))[:, :, None]
    east_cols = shift_cols(tiles, 1)
    west_cols = shift_cols(tiles, -1)
    zonal_diff = (east_cols - west_cols) / (2.0 * cos_centre)
    merid_diff = 0.5 * (north_rows - south_rows)
    advect = wind_u * zonal_diff + wind_v * merid_diff
    u_part = slice(0, levels)
    v_part = slice(levels, 2 * levels)
    h_part = slice(2 * levels, 3 * levels)
    t_part = slice(3 * levels, None)
    diverge = zonal_diff[:, u_part] + (
        north_rows[:, v_part] * cos_north - south_rows[:, v_part] * cos_south
    ) / (2.0 * cos_centre)
    zonal_tend = -advect[:, u_part] + coriolis * tiles[:, v_part] - zonal_diff[:, h_part]
    merid_tend = -advect[:, v_part] - coriolis * tiles[:, u_part] - merid_diff[:, h_part]
    height_tend = -advect[:, h_part] - depth[:, None, None] * diverge
    tracer_tend = -advect[:, t_part] + diffusion.reshape(-1)[:, None, None] * (
        north_rows[:, t_part] - 2.0 * tiles[:, t_part] + south_rows[:, t_part]
    )
    return jnp.concatenate([zonal_tend, merid_tend, height_tend, tracer_tend], axis=1)


def trig_pair(rows, cols, length):
    phases = (
        jnp.arange(rows, dtype=jnp.int32)[:, None] * jnp.arange(cols, dtype=jnp.int32)[None, :]
    ) % length
    angles = phases.astype(jnp.float32) * (2.0 * math.pi / length)
    return jnp.cos(angles), jnp.sin(angles)


def mm(spec, left, right):
    return jnp.einsum(spec, left, right, precision=precision)


def dft_tables(outer, lanes):
    total = outer * lanes
    c_o, s_o = trig_pair(outer, outer, outer)
    c_l, s_l = trig_pair(lanes, lanes, lanes)
    tw_c, tw_s = trig_pair(outer, lanes, total)
    first = jnp.concatenate([c_o, -s_o], axis=0)
    last = jnp.concatenate([c_o, -s_o], axis=1) * (1.0 / total)
    fwd = jnp.concatenate(
        [jnp.concatenate([c_l, -s_l], axis=1), jnp.concatenate([s_l, c_l], axis=1)], axis=0
    )
    inv = jnp.concatenate(
        [jnp.concatenate([c_l, s_l], axis=1), jnp.concatenate([-s_l, c_l], axis=1)], axis=0
    )
    return first, last, fwd, inv, tw_c[:, None, :], tw_s[:, None, :]


def filter_tiles(grid, factors, tables):
    first, last, fwd, inv, tw_c, tw_s = tables
    outer, count, lanes = grid.shape
    half = count // 2
    spread = mm("ka,af->kf", first, grid.reshape(outer, count * lanes))
    spread = spread.reshape(2, outer, count, lanes)
    a_re = spread[0][:, :half] - spread[1][:, half:]
    a_im = spread[0][:, half:] + spread[1][:, :half]
    b_re = a_re * tw_c + a_im * tw_s
    b_im = a_im * tw_c - a_re * tw_s
    joined = jnp.concatenate([b_re, b_im], axis=2)
    spectrum = mm("kcb,bq->kcq", joined, fwd) * factors[:, :half]
    back = mm("kcq,qb->kcb", spectrum, inv)
    d_re = back[:, :, :lanes]
    d_im = back[:, :, lanes:]
    e_re = d_re * tw_c - d_im * tw_s
    e_im = d_im * tw_c + d_re * tw_s
    stacked = jnp.stack(
        [jnp.concatenate([e_re, e_im], axis=1), jnp.concatenate([e_im, -e_re], axis=1)], axis=0
    ).reshape(2 * outer, count * lanes)
    return mm("ak,kf->af", last, stacked).reshape(outer, count, lanes)


def slab_path(lon_devs):
    if lon_devs != 16:
        order = list(range(lon_devs))
        if lon_devs >= 4:
            order[2], order[3] = order[3], order[2]
        return order
    path = []
    for y_hi in range(2):
        xs = range(4) if y_hi == 0 else range(3, -1, -1)
        for x in xs:
            cores = (0, 1) if (len(path) // 2) % 2 == 0 else (1, 0)
            for core in cores:
                path.append((y_hi * 4 + x) * 2 + core)
    return path


def local(prognostic, wind_zonal, wind_merid, layer_depth, diffusion):
    field_count, level_count, col_count, row_count = prognostic.shape
    lat_devs = lax.axis_size("lat")
    lon_devs = lax.axis_size("lon")
    lat_total = row_count * lat_devs
    circle_len = col_count * lon_devs
    lat_pos = lax.axis_index("lat")
    lon_pos = lax.axis_index("lon")
    quarter = lat_devs // 4
    is_polar = (lat_pos < quarter) | (lat_pos >= lat_devs - quarter)
    vectors = field_count * level_count
    slab_rows = row_count // lon_devs
    devices = lat_devs * lon_devs
    lanes = 128
    outer = circle_len // lanes
    path = slab_path(lon_devs)
    paths = [path, path[::-1]]
    slots = [[p.index(d) for d in range(lon_devs)] for p in paths]
    parity = lat_pos % 2
    pos_of_slab = jnp.take(jnp.array(paths, dtype=jnp.int32), parity, axis=0)
    slab_of_pos = jnp.take(jnp.array(slots, dtype=jnp.int32), parity, axis=0)
    my_slab = jnp.take(slab_of_pos, lon_pos)
    row_ids = lat_pos * row_count + my_slab * slab_rows + jnp.arange(slab_rows, dtype=jnp.int32)
    winds_u = lax.dynamic_slice_in_dim(wind_zonal, my_slab * slab_rows, slab_rows, axis=1)
    winds_v = lax.dynamic_slice_in_dim(wind_merid, my_slab * slab_rows, slab_rows, axis=1)

    halfway = damping(row_ids, lat_total, circle_len)
    mirrored = halfway[:, 1 : circle_len // 2][:, ::-1]
    full = jnp.concatenate([halfway, mirrored], axis=1)
    by_k = jnp.transpose(full.reshape(slab_rows, lanes, outer), (2, 0, 1))
    by_k = jnp.broadcast_to(by_k[:, None], (outer, vectors, slab_rows, lanes))
    by_k = by_k.reshape(outer, vectors * slab_rows, lanes)
    factors = jnp.concatenate([by_k, by_k], axis=2)
    tables = dft_tables(outer, lanes)

    send = prognostic.reshape(vectors, col_count, lon_devs, slab_rows)
    send = jnp.transpose(send, (2, 1, 0, 3))
    send = jnp.take(send, slab_of_pos, axis=0)
    recv = lax.all_to_all(send, "lon", 0, 0, tiled=True)
    state = jnp.transpose(recv, (2, 3, 0, 1)).reshape(vectors, slab_rows, outer, lanes)
    state = lax.optimization_barrier(jnp.transpose(state, (2, 0, 1, 3)))

    up = []
    for lat in range(lat_devs):
        for slab in range(lon_devs):
            here = lat * lon_devs + paths[lat % 2][slab]
            if slab + 1 < lon_devs:
                up.append((here, lat * lon_devs + paths[lat % 2][slab + 1]))
            elif lat + 1 < lat_devs:
                up.append((here, (lat + 1) * lon_devs + paths[(lat + 1) % 2][0]))
    down = [(b, a) for a, b in up]
    row_pos = jnp.arange(slab_rows, dtype=jnp.int32)[None, None, :, None]
    for substep in range(ITERS):
        south = lax.ppermute(state[:, :, -1, :], ("lat", "lon"), up)
        north = lax.ppermute(state[:, :, 0, :], ("lat", "lon"), down)
        north_rows = jnp.where(
            row_pos == slab_rows - 1, north[:, :, None, :], jnp.roll(state, -1, axis=2)
        )
        south_rows = jnp.where(row_pos == 0, south[:, :, None, :], jnp.roll(state, 1, axis=2))
        tendency_now = tendency(
            state,
            north_rows,
            south_rows,
            row_ids,
            lat_total,
            winds_u,
            winds_v,
            layer_depth,
            diffusion,
        )
        grid = tendency_now.reshape(outer, vectors * slab_rows, lanes)
        filtered = jnp.where(is_polar, filter_tiles(grid, factors, tables), grid)
        state = state + time_step * filtered.reshape(state.shape)

    out = jnp.transpose(lax.optimization_barrier(state), (1, 2, 0, 3))
    out = out.reshape(vectors, slab_rows, lon_devs, col_count)
    out = jnp.transpose(out, (2, 3, 0, 1))
    out = lax.all_to_all(out, "lon", 0, 0, tiled=True)
    out = jnp.take(out, pos_of_slab, axis=0)
    out = jnp.transpose(out, (2, 1, 0, 3)).reshape(prognostic.shape)
    return out


def solution(mesh):
    return jax.shard_map(
        local,
        mesh=mesh,
        in_specs=(P(None, None, "lon", "lat"), P(None, "lat"), P(None, "lat"), P(), P()),
        out_specs=P(None, None, "lon", "lat"),
        check_vma=False,
    )
```

```python
import math

import jax
import jax.numpy as jnp
from jax import lax
from jax.sharding import PartitionSpec as P

ITERS = 3


time_step = 0.15
precision = lax.Precision.HIGH


def latitude(row_ids, lat_total):
    return (row_ids.astype(jnp.float32) + 0.5) * (math.pi / lat_total) - 0.5 * math.pi


def damping(row_ids, lat_total, circle_len):
    cos_ratio = jnp.cos(latitude(row_ids, lat_total)) / math.cos(0.25 * math.pi)
    wave_ids = jnp.arange(circle_len // 2 + 1)
    sine_vals = jnp.sin(wave_ids.astype(jnp.float32) * (math.pi / circle_len))
    safe_sines = jnp.where(wave_ids == 0, 1.0, sine_vals)
    return jnp.where(
        wave_ids[None, :] == 0, 1.0, jnp.minimum(1.0, cos_ratio[:, None] / safe_sines[None, :])
    )


def shift_cols(tiles, step):
    lanes = tiles.shape[3]
    inside = jnp.roll(tiles, -step, axis=3)
    carried = jnp.roll(inside, -step, axis=0)
    lane_ids = jnp.arange(lanes, dtype=jnp.int32)[None, None, None, :]
    edge = lane_ids == (lanes - 1 if step > 0 else 0)
    return jnp.where(edge, carried, inside)


def tendency(tiles, north_rows, south_rows, row_ids, lat_total, winds_u, winds_v, depth, diffusion):
    levels = depth.shape[0]
    fields = tiles.shape[1] // levels
    latitudes = latitude(row_ids, lat_total)[:, None]
    cos_centre = jnp.cos(latitudes)
    cos_north = jnp.cos(latitude(row_ids + 1, lat_total))[:, None]
    cos_south = jnp.cos(latitude(row_ids - 1, lat_total))[:, None]
    coriolis = jnp.sin(latitudes)
    wind_u = jnp.tile(winds_u, (fields, 1))[:, :, None]
    wind_v = jnp.tile(winds_v, (fields, 1))[:, :, None]
    east_cols = shift_cols(tiles, 1)
    west_cols = shift_cols(tiles, -1)
    zonal_diff = (east_cols - west_cols) / (2.0 * cos_centre)
    merid_diff = 0.5 * (north_rows - south_rows)
    advect = wind_u * zonal_diff + wind_v * merid_diff
    u_part = slice(0, levels)
    v_part = slice(levels, 2 * levels)
    h_part = slice(2 * levels, 3 * levels)
    t_part = slice(3 * levels, None)
    diverge = zonal_diff[:, u_part] + (
        north_rows[:, v_part] * cos_north - south_rows[:, v_part] * cos_south
    ) / (2.0 * cos_centre)
    zonal_tend = -advect[:, u_part] + coriolis * tiles[:, v_part] - zonal_diff[:, h_part]
    merid_tend = -advect[:, v_part] - coriolis * tiles[:, u_part] - merid_diff[:, h_part]
    height_tend = -advect[:, h_part] - depth[:, None, None] * diverge
    tracer_tend = -advect[:, t_part] + diffusion.reshape(-1)[:, None, None] * (
        north_rows[:, t_part] - 2.0 * tiles[:, t_part] + south_rows[:, t_part]
    )
    return jnp.concatenate([zonal_tend, merid_tend, height_tend, tracer_tend], axis=1)


def trig_pair(rows, cols, length):
    phases = (
        jnp.arange(rows, dtype=jnp.int32)[:, None] * jnp.arange(cols, dtype=jnp.int32)[None, :]
    ) % length
    angles = phases.astype(jnp.float32) * (2.0 * math.pi / length)
    return jnp.cos(angles), jnp.sin(angles)


def mm(spec, left, right):
    return jnp.einsum(spec, left, right, precision=precision)


def dft_tables(outer, lanes):
    total = outer * lanes
    c_o, s_o = trig_pair(outer, outer, outer)
    c_l, s_l = trig_pair(lanes, lanes, lanes)
    tw_c, tw_s = trig_pair(outer, lanes, total)
    first = jnp.concatenate([c_o, -s_o], axis=0)
    last = jnp.concatenate([c_o, -s_o], axis=1) * (1.0 / total)
    fwd = jnp.concatenate(
        [jnp.concatenate([c_l, -s_l], axis=1), jnp.concatenate([s_l, c_l], axis=1)], axis=0
    )
    inv = jnp.concatenate(
        [jnp.concatenate([c_l, s_l], axis=1), jnp.concatenate([-s_l, c_l], axis=1)], axis=0
    )
    return first, last, fwd, inv, tw_c[:, None, :], tw_s[:, None, :]


def filter_tiles(grid, factors, tables):
    first, last, fwd, inv, tw_c, tw_s = tables
    outer, count, lanes = grid.shape
    half = count // 2
    spread = mm("ka,af->kf", first, grid.reshape(outer, count * lanes))
    spread = spread.reshape(2, outer, count, lanes)
    a_re = spread[0][:, :half] - spread[1][:, half:]
    a_im = spread[0][:, half:] + spread[1][:, :half]
    b_re = a_re * tw_c + a_im * tw_s
    b_im = a_im * tw_c - a_re * tw_s
    joined = jnp.concatenate([b_re, b_im], axis=2)
    spectrum = mm("kcb,bq->kcq", joined, fwd) * factors[:, :half]
    back = mm("kcq,qb->kcb", spectrum, inv)
    d_re = back[:, :, :lanes]
    d_im = back[:, :, lanes:]
    e_re = d_re * tw_c - d_im * tw_s
    e_im = d_im * tw_c + d_re * tw_s
    stacked = jnp.stack(
        [jnp.concatenate([e_re, e_im], axis=1), jnp.concatenate([e_im, -e_re], axis=1)], axis=0
    ).reshape(2 * outer, count * lanes)
    return mm("ak,kf->af", last, stacked).reshape(outer, count, lanes)


def slab_path(lon_devs):
    if lon_devs != 16:
        order = list(range(lon_devs))
        if lon_devs >= 4:
            order[2], order[3] = order[3], order[2]
        return order
    path = []
    for y_hi in range(2):
        xs = range(4) if y_hi == 0 else range(3, -1, -1)
        for x in xs:
            cores = (0, 1) if (len(path) // 2) % 2 == 0 else (1, 0)
            for core in cores:
                path.append((y_hi * 4 + x) * 2 + core)
    return path


def local(prognostic, wind_zonal, wind_merid, layer_depth, diffusion):
    field_count, level_count, col_count, row_count = prognostic.shape
    lat_devs = lax.axis_size("lat")
    lon_devs = lax.axis_size("lon")
    lat_total = row_count * lat_devs
    circle_len = col_count * lon_devs
    lat_pos = lax.axis_index("lat")
    lon_pos = lax.axis_index("lon")
    quarter = lat_devs // 4
    is_polar = (lat_pos < quarter) | (lat_pos >= lat_devs - quarter)
    vectors = field_count * level_count
    slab_rows = row_count // lon_devs
    devices = lat_devs * lon_devs
    lanes = 128
    outer = circle_len // lanes
    path = slab_path(lon_devs)
    paths = [path, path[::-1]]
    slots = [[p.index(d) for d in range(lon_devs)] for p in paths]
    parity = lat_pos % 2
    pos_of_slab = jnp.take(jnp.array(paths, dtype=jnp.int32), parity, axis=0)
    slab_of_pos = jnp.take(jnp.array(slots, dtype=jnp.int32), parity, axis=0)
    my_slab = jnp.take(slab_of_pos, lon_pos)
    row_ids = lat_pos * row_count + my_slab * slab_rows + jnp.arange(slab_rows, dtype=jnp.int32)
    winds_u = lax.dynamic_slice_in_dim(wind_zonal, my_slab * slab_rows, slab_rows, axis=1)
    winds_v = lax.dynamic_slice_in_dim(wind_merid, my_slab * slab_rows, slab_rows, axis=1)

    halfway = damping(row_ids, lat_total, circle_len)
    mirrored = halfway[:, 1 : circle_len // 2][:, ::-1]
    full = jnp.concatenate([halfway, mirrored], axis=1)
    by_k = jnp.transpose(full.reshape(slab_rows, lanes, outer), (2, 0, 1))
    by_k = jnp.broadcast_to(by_k[:, None], (outer, vectors, slab_rows, lanes))
    by_k = by_k.reshape(outer, vectors * slab_rows, lanes)
    factors = jnp.concatenate([by_k, by_k], axis=2)
    tables = dft_tables(outer, lanes)

    send = prognostic.reshape(vectors, col_count, lon_devs, slab_rows)
    send = jnp.transpose(send, (2, 1, 0, 3))
    send = jnp.where(
        parity == 0, send[jnp.array(slots[0])], send[jnp.array(slots[1])]
    )
    recv = lax.all_to_all(send, "lon", 0, 0, tiled=True)
    state = jnp.transpose(recv, (2, 3, 0, 1)).reshape(vectors, slab_rows, outer, lanes)
    state = lax.optimization_barrier(jnp.transpose(state, (2, 0, 1, 3)))

    up = []
    for lat in range(lat_devs):
        for slab in range(lon_devs):
            here = lat * lon_devs + paths[lat % 2][slab]
            if slab + 1 < lon_devs:
                up.append((here, lat * lon_devs + paths[lat % 2][slab + 1]))
            elif lat + 1 < lat_devs:
                up.append((here, (lat + 1) * lon_devs + paths[(lat + 1) % 2][0]))
    down = [(b, a) for a, b in up]
    row_pos = jnp.arange(slab_rows, dtype=jnp.int32)[None, None, :, None]
    for substep in range(ITERS):
        south = lax.ppermute(state[:, :, -1, :], ("lat", "lon"), up)
        north = lax.ppermute(state[:, :, 0, :], ("lat", "lon"), down)
        north_rows = jnp.where(
            row_pos == slab_rows - 1, north[:, :, None, :], jnp.roll(state, -1, axis=2)
        )
        south_rows = jnp.where(row_pos == 0, south[:, :, None, :], jnp.roll(state, 1, axis=2))
        tendency_now = tendency(
            state,
            north_rows,
            south_rows,
            row_ids,
            lat_total,
            winds_u,
            winds_v,
            layer_depth,
            diffusion,
        )
        grid = tendency_now.reshape(outer, vectors * slab_rows, lanes)
        filtered = jnp.where(is_polar, filter_tiles(grid, factors, tables), grid)
        state = state + time_step * filtered.reshape(state.shape)

    out = jnp.transpose(lax.optimization_barrier(state), (1, 2, 0, 3))
    out = out.reshape(vectors, slab_rows, lon_devs, col_count)
    out = jnp.transpose(out, (2, 3, 0, 1))
    out = lax.all_to_all(out, "lon", 0, 0, tiled=True)
    out = jnp.where(parity == 0, out[jnp.array(paths[0])], out[jnp.array(paths[1])])
    out = jnp.transpose(out, (2, 1, 0, 3)).reshape(prognostic.shape)
    return out


def solution(mesh):
    return jax.shard_map(
        local,
        mesh=mesh,
        in_specs=(P(None, None, "lon", "lat"), P(None, "lat"), P(None, "lat"), P(), P()),
        out_specs=P(None, None, "lon", "lat"),
        check_vma=False,
    )
```

```python
import math

import jax
import jax.numpy as jnp
from jax import lax
from jax.sharding import PartitionSpec as P

ITERS = 3


time_step = 0.15
precision = lax.Precision.HIGH


def latitude(row_ids, lat_total):
    return (row_ids.astype(jnp.float32) + 0.5) * (math.pi / lat_total) - 0.5 * math.pi


def damping(row_ids, lat_total, circle_len):
    cos_ratio = jnp.cos(latitude(row_ids, lat_total)) / math.cos(0.25 * math.pi)
    wave_ids = jnp.arange(circle_len // 2 + 1)
    sine_vals = jnp.sin(wave_ids.astype(jnp.float32) * (math.pi / circle_len))
    safe_sines = jnp.where(wave_ids == 0, 1.0, sine_vals)
    return jnp.where(
        wave_ids[None, :] == 0, 1.0, jnp.minimum(1.0, cos_ratio[:, None] / safe_sines[None, :])
    )


def shift_cols(tiles, step):
    lanes = tiles.shape[3]
    inside = jnp.roll(tiles, -step, axis=3)
    carried = jnp.roll(inside, -step, axis=0)
    lane_ids = jnp.arange(lanes, dtype=jnp.int32)[None, None, None, :]
    edge = lane_ids == (lanes - 1 if step > 0 else 0)
    return jnp.where(edge, carried, inside)


def tendency(tiles, north_rows, south_rows, row_ids, lat_total, winds_u, winds_v, depth, diffusion):
    levels = depth.shape[0]
    fields = tiles.shape[1] // levels
    latitudes = latitude(row_ids, lat_total)[:, None]
    cos_centre = jnp.cos(latitudes)
    cos_north = jnp.cos(latitude(row_ids + 1, lat_total))[:, None]
    cos_south = jnp.cos(latitude(row_ids - 1, lat_total))[:, None]
    coriolis = jnp.sin(latitudes)
    wind_u = jnp.tile(winds_u, (fields, 1))[:, :, None]
    wind_v = jnp.tile(winds_v, (fields, 1))[:, :, None]
    east_cols = shift_cols(tiles, 1)
    west_cols = shift_cols(tiles, -1)
    zonal_diff = (east_cols - west_cols) / (2.0 * cos_centre)
    merid_diff = 0.5 * (north_rows - south_rows)
    advect = wind_u * zonal_diff + wind_v * merid_diff
    u_part = slice(0, levels)
    v_part = slice(levels, 2 * levels)
    h_part = slice(2 * levels, 3 * levels)
    t_part = slice(3 * levels, None)
    diverge = zonal_diff[:, u_part] + (
        north_rows[:, v_part] * cos_north - south_rows[:, v_part] * cos_south
    ) / (2.0 * cos_centre)
    zonal_tend = -advect[:, u_part] + coriolis * tiles[:, v_part] - zonal_diff[:, h_part]
    merid_tend = -advect[:, v_part] - coriolis * tiles[:, u_part] - merid_diff[:, h_part]
    height_tend = -advect[:, h_part] - depth[:, None, None] * diverge
    tracer_tend = -advect[:, t_part] + diffusion.reshape(-1)[:, None, None] * (
        north_rows[:, t_part] - 2.0 * tiles[:, t_part] + south_rows[:, t_part]
    )
    return jnp.concatenate([zonal_tend, merid_tend, height_tend, tracer_tend], axis=1)


def trig_pair(rows, cols, length):
    phases = (
        jnp.arange(rows, dtype=jnp.int32)[:, None] * jnp.arange(cols, dtype=jnp.int32)[None, :]
    ) % length
    angles = phases.astype(jnp.float32) * (2.0 * math.pi / length)
    return jnp.cos(angles), jnp.sin(angles)


def mm(spec, left, right):
    return jnp.einsum(spec, left, right, precision=precision)


def dft_tables(outer, lanes):
    total = outer * lanes
    c_o, s_o = trig_pair(outer, outer, outer)
    c_l, s_l = trig_pair(lanes, lanes, lanes)
    tw_c, tw_s = trig_pair(outer, lanes, total)
    first = jnp.concatenate([c_o, -s_o], axis=0)
    last = jnp.concatenate([c_o, -s_o], axis=1) * (1.0 / total)
    fwd = jnp.concatenate(
        [jnp.concatenate([c_l, -s_l], axis=1), jnp.concatenate([s_l, c_l], axis=1)], axis=0
    )
    inv = jnp.concatenate(
        [jnp.concatenate([c_l, s_l], axis=1), jnp.concatenate([-s_l, c_l], axis=1)], axis=0
    )
    return first, last, fwd, inv, tw_c[:, None, :], tw_s[:, None, :]


def filter_tiles(grid, factors, tables):
    first, last, fwd, inv, tw_c, tw_s = tables
    outer, count, lanes = grid.shape
    half = count // 2
    spread = mm("ka,af->kf", first, grid.reshape(outer, count * lanes))
    spread = spread.reshape(2, outer, count, lanes)
    a_re = spread[0][:, :half] - spread[1][:, half:]
    a_im = spread[0][:, half:] + spread[1][:, :half]
    b_re = a_re * tw_c + a_im * tw_s
    b_im = a_im * tw_c - a_re * tw_s
    joined = jnp.concatenate([b_re, b_im], axis=2)
    spectrum = mm("kcb,bq->kcq", joined, fwd) * factors[:, :half]
    back = mm("kcq,qb->kcb", spectrum, inv)
    d_re = back[:, :, :lanes]
    d_im = back[:, :, lanes:]
    e_re = d_re * tw_c - d_im * tw_s
    e_im = d_im * tw_c + d_re * tw_s
    stacked = jnp.stack(
        [jnp.concatenate([e_re, e_im], axis=1), jnp.concatenate([e_im, -e_re], axis=1)], axis=0
    ).reshape(2 * outer, count * lanes)
    return mm("ak,kf->af", last, stacked).reshape(outer, count, lanes)


def slab_path(lon_devs):
    if lon_devs != 16:
        order = list(range(lon_devs))
        if lon_devs >= 4:
            order[2], order[3] = order[3], order[2]
        return order
    path = []
    for y_hi in range(2):
        xs = range(4) if y_hi == 0 else range(3, -1, -1)
        for x in xs:
            cores = (0, 1) if (len(path) // 2) % 2 == 0 else (1, 0)
            for core in cores:
                path.append((y_hi * 4 + x) * 2 + core)
    return path


def local(prognostic, wind_zonal, wind_merid, layer_depth, diffusion):
    field_count, level_count, col_count, row_count = prognostic.shape
    lat_devs = lax.axis_size("lat")
    lon_devs = lax.axis_size("lon")
    lat_total = row_count * lat_devs
    circle_len = col_count * lon_devs
    lat_pos = lax.axis_index("lat")
    lon_pos = lax.axis_index("lon")
    quarter = lat_devs // 4
    is_polar = (lat_pos < quarter) | (lat_pos >= lat_devs - quarter)
    vectors = field_count * level_count
    slab_rows = row_count // lon_devs
    devices = lat_devs * lon_devs
    lanes = 128
    outer = circle_len // lanes
    path = slab_path(lon_devs)
    paths = [path, path[::-1]]
    slots = [[p.index(d) for d in range(lon_devs)] for p in paths]
    parity = lat_pos % 2
    pos_of_slab = jnp.take(jnp.array(paths, dtype=jnp.int32), parity, axis=0)
    slab_of_pos = jnp.take(jnp.array(slots, dtype=jnp.int32), parity, axis=0)
    my_slab = jnp.take(slab_of_pos, lon_pos)
    row_ids = lat_pos * row_count + my_slab * slab_rows + jnp.arange(slab_rows, dtype=jnp.int32)
    winds_u = lax.dynamic_slice_in_dim(wind_zonal, my_slab * slab_rows, slab_rows, axis=1)
    winds_v = lax.dynamic_slice_in_dim(wind_merid, my_slab * slab_rows, slab_rows, axis=1)

    halfway = damping(row_ids, lat_total, circle_len)
    mirrored = halfway[:, 1 : circle_len // 2][:, ::-1]
    full = jnp.concatenate([halfway, mirrored], axis=1)
    by_k = jnp.transpose(full.reshape(slab_rows, lanes, outer), (2, 0, 1))
    by_k = jnp.broadcast_to(by_k[:, None], (outer, vectors, slab_rows, lanes))
    by_k = by_k.reshape(outer, vectors * slab_rows, lanes)
    factors = jnp.concatenate([by_k, by_k], axis=2)
    tables = dft_tables(outer, lanes)

    send = prognostic.reshape(vectors, col_count, lon_devs, slab_rows)
    send = jnp.transpose(send, (2, 1, 0, 3))
    send = jnp.take(send, slab_of_pos, axis=0)
    recv = lax.all_to_all(send, "lon", 0, 0, tiled=True)
    state = jnp.transpose(recv, (2, 3, 0, 1)).reshape(vectors, slab_rows, outer, lanes)
    state = jnp.transpose(state, (2, 0, 1, 3))

    up = []
    for lat in range(lat_devs):
        for slab in range(lon_devs):
            here = lat * lon_devs + paths[lat % 2][slab]
            if slab + 1 < lon_devs:
                up.append((here, lat * lon_devs + paths[lat % 2][slab + 1]))
            elif lat + 1 < lat_devs:
                up.append((here, (lat + 1) * lon_devs + paths[(lat + 1) % 2][0]))
    down = [(b, a) for a, b in up]
    row_pos = jnp.arange(slab_rows, dtype=jnp.int32)[None, None, :, None]
    for substep in range(ITERS):
        south = lax.ppermute(state[:, :, -1, :], ("lat", "lon"), up)
        north = lax.ppermute(state[:, :, 0, :], ("lat", "lon"), down)
        north_rows = jnp.where(
            row_pos == slab_rows - 1, north[:, :, None, :], jnp.roll(state, -1, axis=2)
        )
        south_rows = jnp.where(row_pos == 0, south[:, :, None, :], jnp.roll(state, 1, axis=2))
        tendency_now = tendency(
            state,
            north_rows,
            south_rows,
            row_ids,
            lat_total,
            winds_u,
            winds_v,
            layer_depth,
            diffusion,
        )
        grid = tendency_now.reshape(outer, vectors * slab_rows, lanes)
        filtered = jnp.where(is_polar, filter_tiles(grid, factors, tables), grid)
        state = state + time_step * filtered.reshape(state.shape)

    out = jnp.transpose(lax.optimization_barrier(state), (1, 2, 0, 3))
    out = out.reshape(vectors, slab_rows, lon_devs, col_count)
    out = jnp.transpose(out, (2, 3, 0, 1))
    out = lax.all_to_all(out, "lon", 0, 0, tiled=True)
    out = jnp.take(out, pos_of_slab, axis=0)
    out = jnp.transpose(out, (2, 1, 0, 3)).reshape(prognostic.shape)
    return out


def solution(mesh):
    return jax.shard_map(
        local,
        mesh=mesh,
        in_specs=(P(None, None, "lon", "lat"), P(None, "lat"), P(None, "lat"), P(), P()),
        out_specs=P(None, None, "lon", "lat"),
        check_vma=False,
    )
```

```python
import math

import jax
import jax.numpy as jnp
from jax import lax
from jax.sharding import PartitionSpec as P

ITERS = 3


time_step = 0.15
precision = lax.Precision.HIGH


def latitude(row_ids, lat_total):
    return (row_ids.astype(jnp.float32) + 0.5) * (math.pi / lat_total) - 0.5 * math.pi


def damping(row_ids, lat_total, circle_len):
    cos_ratio = jnp.cos(latitude(row_ids, lat_total)) / math.cos(0.25 * math.pi)
    wave_ids = jnp.arange(circle_len // 2 + 1)
    sine_vals = jnp.sin(wave_ids.astype(jnp.float32) * (math.pi / circle_len))
    safe_sines = jnp.where(wave_ids == 0, 1.0, sine_vals)
    return jnp.where(
        wave_ids[None, :] == 0, 1.0, jnp.minimum(1.0, cos_ratio[:, None] / safe_sines[None, :])
    )


def shift_cols(tiles, step):
    lanes = tiles.shape[3]
    inside = jnp.roll(tiles, -step, axis=3)
    carried = jnp.roll(inside, -step, axis=0)
    lane_ids = jnp.arange(lanes, dtype=jnp.int32)[None, None, None, :]
    edge = lane_ids == (lanes - 1 if step > 0 else 0)
    return jnp.where(edge, carried, inside)


def tendency(tiles, north_rows, south_rows, row_ids, lat_total, winds_u, winds_v, depth, diffusion):
    levels = depth.shape[0]
    fields = tiles.shape[1] // levels
    latitudes = latitude(row_ids, lat_total)[:, None]
    cos_centre = jnp.cos(latitudes)
    cos_north = jnp.cos(latitude(row_ids + 1, lat_total))[:, None]
    cos_south = jnp.cos(latitude(row_ids - 1, lat_total))[:, None]
    coriolis = jnp.sin(latitudes)
    wind_u = jnp.tile(winds_u, (fields, 1))[:, :, None]
    wind_v = jnp.tile(winds_v, (fields, 1))[:, :, None]
    east_cols = shift_cols(tiles, 1)
    west_cols = shift_cols(tiles, -1)
    zonal_diff = (east_cols - west_cols) / (2.0 * cos_centre)
    merid_diff = 0.5 * (north_rows - south_rows)
    advect = wind_u * zonal_diff + wind_v * merid_diff
    u_part = slice(0, levels)
    v_part = slice(levels, 2 * levels)
    h_part = slice(2 * levels, 3 * levels)
    t_part = slice(3 * levels, None)
    diverge = zonal_diff[:, u_part] + (
        north_rows[:, v_part] * cos_north - south_rows[:, v_part] * cos_south
    ) / (2.0 * cos_centre)
    zonal_tend = -advect[:, u_part] + coriolis * tiles[:, v_part] - zonal_diff[:, h_part]
    merid_tend = -advect[:, v_part] - coriolis * tiles[:, u_part] - merid_diff[:, h_part]
    height_tend = -advect[:, h_part] - depth[:, None, None] * diverge
    tracer_tend = -advect[:, t_part] + diffusion.reshape(-1)[:, None, None] * (
        north_rows[:, t_part] - 2.0 * tiles[:, t_part] + south_rows[:, t_part]
    )
    return jnp.concatenate([zonal_tend, merid_tend, height_tend, tracer_tend], axis=1)


def trig_pair(rows, cols, length):
    phases = (
        jnp.arange(rows, dtype=jnp.int32)[:, None] * jnp.arange(cols, dtype=jnp.int32)[None, :]
    ) % length
    angles = phases.astype(jnp.float32) * (2.0 * math.pi / length)
    return jnp.cos(angles), jnp.sin(angles)


def mm(spec, left, right):
    return jnp.einsum(spec, left, right, precision=precision)


def dft_tables(outer, lanes):
    total = outer * lanes
    c_o, s_o = trig_pair(outer, outer, outer)
    c_l, s_l = trig_pair(lanes, lanes, lanes)
    tw_c, tw_s = trig_pair(outer, lanes, total)
    first = jnp.concatenate([c_o, -s_o], axis=0)
    last = jnp.concatenate([c_o, -s_o], axis=1) * (1.0 / total)
    fwd = jnp.concatenate(
        [jnp.concatenate([c_l, -s_l], axis=1), jnp.concatenate([s_l, c_l], axis=1)], axis=0
    )
    inv = jnp.concatenate(
        [jnp.concatenate([c_l, s_l], axis=1), jnp.concatenate([-s_l, c_l], axis=1)], axis=0
    )
    return first, last, fwd, inv, tw_c[:, None, :], tw_s[:, None, :]


def filter_tiles(grid, factors, tables):
    first, last, fwd, inv, tw_c, tw_s = tables
    outer, count, lanes = grid.shape
    half = count // 2
    spread = mm("ka,af->kf", first, grid.reshape(outer, count * lanes))
    spread = spread.reshape(2, outer, count, lanes)
    a_re = spread[0][:, :half] - spread[1][:, half:]
    a_im = spread[0][:, half:] + spread[1][:, :half]
    b_re = a_re * tw_c + a_im * tw_s
    b_im = a_im * tw_c - a_re * tw_s
    joined = jnp.concatenate([b_re, b_im], axis=2)
    spectrum = mm("kcb,bq->kcq", joined, fwd) * factors[:, :half]
    back = mm("kcq,qb->kcb", spectrum, inv)
    d_re = back[:, :, :lanes]
    d_im = back[:, :, lanes:]
    e_re = d_re * tw_c - d_im * tw_s
    e_im = d_im * tw_c + d_re * tw_s
    stacked = jnp.stack(
        [jnp.concatenate([e_re, e_im], axis=1), jnp.concatenate([e_im, -e_re], axis=1)], axis=0
    ).reshape(2 * outer, count * lanes)
    return mm("ak,kf->af", last, stacked).reshape(outer, count, lanes)


def slab_path(lon_devs):
    if lon_devs != 16:
        order = list(range(lon_devs))
        if lon_devs >= 4:
            order[2], order[3] = order[3], order[2]
        return order
    path = []
    for y_hi in range(2):
        xs = range(4) if y_hi == 0 else range(3, -1, -1)
        for x in xs:
            cores = (0, 1) if (len(path) // 2) % 2 == 0 else (1, 0)
            for core in cores:
                path.append((y_hi * 4 + x) * 2 + core)
    return path


def local(prognostic, wind_zonal, wind_merid, layer_depth, diffusion):
    field_count, level_count, col_count, row_count = prognostic.shape
    lat_devs = lax.axis_size("lat")
    lon_devs = lax.axis_size("lon")
    lat_total = row_count * lat_devs
    circle_len = col_count * lon_devs
    lat_pos = lax.axis_index("lat")
    lon_pos = lax.axis_index("lon")
    quarter = lat_devs // 4
    is_polar = (lat_pos < quarter) | (lat_pos >= lat_devs - quarter)
    vectors = field_count * level_count
    slab_rows = row_count // lon_devs
    devices = lat_devs * lon_devs
    lanes = 128
    outer = circle_len // lanes
    path = slab_path(lon_devs)
    paths = [path, path[::-1]]
    slots = [[p.index(d) for d in range(lon_devs)] for p in paths]
    parity = lat_pos % 2
    pos_of_slab = jnp.take(jnp.array(paths, dtype=jnp.int32), parity, axis=0)
    slab_of_pos = jnp.take(jnp.array(slots, dtype=jnp.int32), parity, axis=0)
    my_slab = jnp.take(slab_of_pos, lon_pos)
    row_ids = lat_pos * row_count + my_slab * slab_rows + jnp.arange(slab_rows, dtype=jnp.int32)
    winds_u = lax.dynamic_slice_in_dim(wind_zonal, my_slab * slab_rows, slab_rows, axis=1)
    winds_v = lax.dynamic_slice_in_dim(wind_merid, my_slab * slab_rows, slab_rows, axis=1)

    halfway = damping(row_ids, lat_total, circle_len)
    mirrored = halfway[:, 1 : circle_len // 2][:, ::-1]
    full = jnp.concatenate([halfway, mirrored], axis=1)
    by_k = jnp.transpose(full.reshape(slab_rows, lanes, outer), (2, 0, 1))
    by_k = jnp.broadcast_to(by_k[:, None], (outer, vectors, slab_rows, lanes))
    by_k = by_k.reshape(outer, vectors * slab_rows, lanes)
    factors = jnp.concatenate([by_k, by_k], axis=2)
    tables = dft_tables(outer, lanes)

    send = prognostic.reshape(vectors, col_count, lon_devs, slab_rows)
    send = jnp.transpose(send, (2, 1, 0, 3))
    send = jnp.take(send, slab_of_pos, axis=0)
    recv = lax.all_to_all(send, "lon", 0, 0, tiled=True)
    state = jnp.transpose(recv, (2, 3, 0, 1)).reshape(vectors, slab_rows, outer, lanes)
    state = jnp.transpose(state, (2, 0, 1, 3))

    up = []
    for lat in range(lat_devs):
        for slab in range(lon_devs):
            here = lat * lon_devs + paths[lat % 2][slab]
            if slab + 1 < lon_devs:
                up.append((here, lat * lon_devs + paths[lat % 2][slab + 1]))
            elif lat + 1 < lat_devs:
                up.append((here, (lat + 1) * lon_devs + paths[(lat + 1) % 2][0]))
    down = [(b, a) for a, b in up]
    row_pos = jnp.arange(slab_rows, dtype=jnp.int32)[None, None, :, None]
    for substep in range(ITERS):
        south = lax.ppermute(state[:, :, -1, :], ("lat", "lon"), up)
        north = lax.ppermute(state[:, :, 0, :], ("lat", "lon"), down)
        north_rows = jnp.where(
            row_pos == slab_rows - 1, north[:, :, None, :], jnp.roll(state, -1, axis=2)
        )
        south_rows = jnp.where(row_pos == 0, south[:, :, None, :], jnp.roll(state, 1, axis=2))
        tendency_now = tendency(
            state,
            north_rows,
            south_rows,
            row_ids,
            lat_total,
            winds_u,
            winds_v,
            layer_depth,
            diffusion,
        )
        grid = tendency_now.reshape(outer, vectors * slab_rows, lanes)
        filtered = jnp.where(is_polar, filter_tiles(grid, factors, tables), grid)
        state = state + time_step * filtered.reshape(state.shape)

    out = jnp.transpose(state, (1, 2, 0, 3))
    out = out.reshape(vectors, slab_rows, lon_devs, col_count)
    out = jnp.transpose(out, (2, 3, 0, 1))
    out = lax.all_to_all(out, "lon", 0, 0, tiled=True)
    out = jnp.take(out, pos_of_slab, axis=0)
    out = jnp.transpose(out, (2, 1, 0, 3)).reshape(prognostic.shape)
    return out


def solution(mesh):
    return jax.shard_map(
        local,
        mesh=mesh,
        in_specs=(P(None, None, "lon", "lat"), P(None, "lat"), P(None, "lat"), P(), P()),
        out_specs=P(None, None, "lon", "lat"),
        check_vma=False,
    )
```
